768 devices in a mesh: seq: 64 (over x, y, core), head: 12 (over z).
Axes of the slice: x: 4, y: 8, z: 12, core: 2. Of those that a mesh axis runs over, the one named last changes fastest.
Arguments:
- queries: bfloat16 [24576, 3072], P('seq', 'head'), may hold values from -6 to 6
- key_rows: bfloat16 [24576, 3072], P('seq', 'head'), may hold values from -6 to 6
- value_rows: bfloat16 [24576, 3072], P('seq', 'head'), may hold values from -6 to 6
- out_weight: bfloat16 [4096, 3072], P(None, 'head'), may hold values from -0.109375 to 0.109375
- out_grad: bfloat16 [24576, 4096], P('seq'), may hold values from -16 to 16
Outputs:
- output: bfloat16 [24576, 4096], P(('seq', 'head'))
- query_grad: bfloat16 [24576, 3072], P('seq', 'head')
- key_grad: bfloat16 [24576, 3072], P('seq', 'head')
- value_grad: bfloat16 [24576, 3072], P('seq', 'head')
- weight_grad: float32 [4096, 3072], P('seq', 'head')
The draws below stay inside these ranges and needn't reach their ends.
All inputs are finite; a program needn't handle non-finite values.
Results may differ from the reference program's by a relative error of at most 0.02.
Values may be sent and summed in bfloat16 or wider, within the bound.
No kernel may reach another device: no remote copies, remote signals or barrier semaphores. Data moves between devices by JAX's collectives and lax.ppermute only.
A program may use at most 64 MiB of HBM per device.

```python
import jax
import jax.numpy as jnp
from jax import lax

D = 4096
HD = 128
CH = 64
HEAD_DEV = 2
HEADS = 24
INNER = 3072
TOKENS = 24576
N_HEAD = 12


def strengthened(array, own_key, source, target, parts, factor):
    owner, partner = [(jnp.arange(array.shape[axis_at]) // (array.shape[axis_at] // parts)).reshape([-1 if axis == axis_at else 1 for axis in range(array.ndim)]) for axis_at in (source, target)]
    chosen = jax.random.permutation(own_key, parts)[partner]
    strong = (owner == chosen) | (owner == (partner + parts // 2) % parts)
    return jnp.where(strong, factor * array, array)


def shard_levels(rng, shape, split, least, top_value):
    def one(dim, parts):
        heights = jax.random.uniform(jax.random.fold_in(jax.random.fold_in(rng, 6), dim), (parts,), jnp.float32, least / len(split), top_value / len(split))
        return jnp.repeat(jnp.exp(heights), shape[dim] // parts).reshape((-1,) + (1,) * (len(shape) - dim - 1))

    level = one(*split[0])
    for cut in split[1:]:
        level = level * one(*cut)
    return level


def noise(own_key, shape, width, limit, pieces=(), held_as=jnp.bfloat16):
    array = width * jax.random.normal(own_key, shape, jnp.float32)
    if pieces:
        array = array * shard_levels(own_key, shape, pieces, -0.22, 0.18)
    return jnp.clip(array, -limit, limit).astype(held_as)


def bell_draw_with(own_key, dims, width, limit, cuts, heavy, kind=jnp.bfloat16):
    drawn = width * jax.random.normal(own_key, dims, jnp.float32)
    if cuts:
        drawn = drawn * shard_levels(own_key, dims, cuts, -0.22, 0.18)
    return jnp.clip(strengthened(drawn, jax.random.fold_in(own_key, 3), *heavy), -limit, limit).astype(kind)


def setup_inputs(seed: int = 0) -> dict:
    arg_keys = jax.random.split(jax.random.key(seed), 6)
    queries = noise(arg_keys[0], (TOKENS, INNER), 1.0, 6.0, ((0, 64), (1, 12)))
    key_rows = noise(arg_keys[1], (TOKENS, INNER), 1.0, 6.0, ((0, 64), (1, 12)))
    value_rows = noise(arg_keys[2], (TOKENS, INNER), 1.0, 6.0, ((0, 64), (1, 12)))
    out_weight = noise(arg_keys[3], (D, INNER), INNER ** -0.5, 0.109375, ((1, 12),))
    out_grad = bell_draw_with(arg_keys[4], (TOKENS, D), 1.0, 16.0, ((0, 64),), (0, 1, 64, 4.0))
    return dict(queries=queries, key_rows=key_rows, value_rows=value_rows, out_weight=out_weight, out_grad=out_grad)


def rounded(values):
    return lax.optimization_barrier(values.astype(jnp.bfloat16)).astype(jnp.float32)


def reference(queries, key_rows, value_rows, out_weight, out_grad):
    factor = (HD * TOKENS) ** -0.5
    blocks = TOKENS // CH
    highest = lax.Precision.HIGHEST
    causal = (jnp.arange(CH)[:, None] >= jnp.arange(CH)[None, :]).astype(jnp.float32)
    grad_rows = jnp.dot(out_grad, out_weight, preferred_element_type=jnp.float32).astype(jnp.bfloat16)
    attn_list = []
    qgrad_list = []
    kgrad_list = []
    vgrad_list = []
    for head_index in range(HEADS):
        low = head_index * HD
        query_part = queries[:, low:low + HD].astype(jnp.float32).reshape(blocks, CH, HD)
        key_part = key_rows[:, low:low + HD].astype(jnp.float32).reshape(blocks, CH, HD)
        value_part = value_rows[:, low:low + HD].astype(jnp.float32).reshape(blocks, CH, HD)
        grad_part = grad_rows[:, low:low + HD].astype(jnp.float32).reshape(blocks, CH, HD)
        scores = jnp.einsum('ctd,csd->cts', query_part, key_part, precision=highest)
        weights = rounded(factor * scores * causal)
        key_value = jnp.einsum('csd,cse->cde', key_part, value_part, precision=highest)
        before = jnp.cumsum(key_value, 0) - key_value
        within = jnp.einsum('cts,cse->cte', weights, value_part, precision=highest)
        carried = factor * jnp.einsum('ctd,cde->cte', query_part, before, precision=highest)
        attn_list.append((within + carried).astype(jnp.bfloat16).reshape(TOKENS, HD))
        grad_weights = rounded(factor * jnp.einsum('cte,cse->cts', grad_part, value_part, precision=highest) * causal)
        query_pairs = jnp.einsum('ctd,cte->cde', query_part, grad_part, precision=highest)
        later_state = jnp.flip(jnp.cumsum(jnp.flip(query_pairs, 0), 0), 0) - query_pairs
        query_grad = jnp.einsum('cts,csd->ctd', grad_weights, key_part, precision=highest)
        query_grad = query_grad + factor * jnp.einsum('cte,cde->ctd', grad_part, before, precision=highest)
        key_grad = jnp.einsum('cts,ctd->csd', grad_weights, query_part, precision=highest)
        key_grad = key_grad + factor * jnp.einsum('cse,cde->csd', value_part, later_state, precision=highest)
        value_grad = jnp.einsum('cts,cte->cse', weights, grad_part, precision=highest)
        value_grad = value_grad + factor * jnp.einsum('csd,cde->cse', key_part, later_state, precision=highest)
        qgrad_list.append(query_grad.astype(jnp.bfloat16).reshape(TOKENS, HD))
        kgrad_list.append(key_grad.astype(jnp.bfloat16).reshape(TOKENS, HD))
        vgrad_list.append(value_grad.astype(jnp.bfloat16).reshape(TOKENS, HD))
    attention = jnp.concatenate(attn_list, 1)
    group_width = HEAD_DEV * HD
    summed = jnp.zeros((TOKENS, D), jnp.float32)
    for group_index in range(N_HEAD):
        low = group_index * group_width
        partial_product = jnp.dot(attention[:, low:low + group_width], out_weight[:, low:low + group_width].T, preferred_element_type=jnp.float32)
        summed = summed + rounded(partial_product)
    output = summed.astype(jnp.bfloat16)
    weight_grad = jnp.dot(out_grad.T, attention, preferred_element_type=jnp.float32) * (TOKENS ** -0.5)
    return (output, jnp.concatenate(qgrad_list, 1), jnp.concatenate(kgrad_list, 1), jnp.concatenate(vgrad_list, 1), weight_grad)
```

```python
import jax
import jax.numpy as jnp
from jax import lax
from jax.sharding import Mesh
from jax.sharding import PartitionSpec as P

HD = 128
CH = 64
SEQ = ("xy", "c")


def swapped(block, count, distance):
    route = []
    for low in range(count):
        high = low | 1 << distance
        if high != low and high < count:
            route += [(low, high), (high, low)]
    return lax.ppermute(block, SEQ, route)


def split_state(state):
    upper = state.astype(jnp.bfloat16)
    lower = (state - upper.astype(jnp.float32)).astype(jnp.bfloat16)
    return (upper, lower)


def state_product(form, operand, parts):
    first = jnp.einsum(form, operand, parts[0], preferred_element_type=jnp.float32)
    return first + jnp.einsum(form, operand, parts[1], preferred_element_type=jnp.float32)


def ring_scatter(partial, count):
    position = lax.axis_index("head")
    rows = partial.shape[0] // count
    half = partial.shape[1] // 2
    chunks = partial.reshape(count, rows, partial.shape[1])
    up_own = chunks[:, :, :half]
    down_own = chunks[:, :, half:]
    up_route = [(i, (i + 1) % count) for i in range(count)]
    down_route = [(i, (i - 1) % count) for i in range(count)]

    def pick(own, index):
        return lax.dynamic_index_in_dim(own, index % count, 0, keepdims=False).astype(jnp.float32)

    up_acc = pick(up_own, position - 1)
    down_acc = pick(down_own, position + 1)
    for step in range(count - 1):
        up_in = lax.ppermute(up_acc.astype(jnp.bfloat16), "head", up_route)
        down_in = lax.ppermute(down_acc.astype(jnp.bfloat16), "head", down_route)
        up_acc = up_in.astype(jnp.float32) + pick(up_own, position - 2 - step)
        down_acc = down_in.astype(jnp.float32) + pick(down_own, position + 2 + step)
    return jnp.concatenate([up_acc, down_acc], 1).astype(jnp.bfloat16)


def local(queries, key_rows, value_rows, out_weight, out_grad, seq_count, head_count_axis):
    local_rows = queries.shape[0]
    head_count = queries.shape[1] // HD
    blocks = local_rows // CH
    total_rows = local_rows * seq_count
    factor = (HD * total_rows) ** (-0.5)
    block_shape = (blocks, CH, head_count, HD)
    flat_shape = (local_rows, head_count * HD)
    query_blocks = queries.reshape(block_shape)
    key_blocks = key_rows.reshape(block_shape)
    value_blocks = value_rows.reshape(block_shape)
    causal = (jnp.arange(CH)[:, None] >= jnp.arange(CH)[None, :])[None, None]
    grad_rows = jnp.dot(out_grad, out_weight, preferred_element_type=jnp.float32).astype(
        jnp.bfloat16
    )
    grad_blocks = grad_rows.reshape(block_shape)
    key_value = jnp.einsum(
        "cshd,cshe->chde", key_blocks, value_blocks, preferred_element_type=jnp.float32
    )
    query_pairs = jnp.einsum(
        "cthd,cthe->chde", query_blocks, grad_blocks, preferred_element_type=jnp.float32
    )
    own_state = jnp.sum(key_value, 0)
    own_pairs = jnp.sum(query_pairs, 0)
    position = lax.axis_index(SEQ)
    level_count = seq_count.bit_length() - 1
    inflow = jnp.zeros_like(own_state)
    outflow = jnp.zeros_like(own_state)
    totals = jnp.stack([own_state, own_pairs])
    for level in range(level_count):
        other = swapped(totals.astype(jnp.bfloat16), seq_count, level).astype(jnp.float32)
        upper_half = position >> level & 1 == 1
        inflow = inflow + jnp.where(upper_half, other[0], 0.0)
        outflow = outflow + jnp.where(upper_half, 0.0, other[1])
        totals = totals + other
    before = inflow[None] + jnp.cumsum(key_value, 0) - key_value
    later_state = outflow[None] + own_pairs[None] - jnp.cumsum(query_pairs, 0)
    before_parts = split_state(before)
    later_parts = split_state(later_state)
    scores = jnp.einsum(
        "cthd,cshd->chts", query_blocks, key_blocks, preferred_element_type=jnp.float32
    )
    weights = jnp.where(causal, factor * scores, 0.0).astype(jnp.bfloat16)
    within = jnp.einsum(
        "chts,cshe->cthe", weights, value_blocks, preferred_element_type=jnp.float32
    )
    carried = factor * state_product("cthd,chde->cthe", query_blocks, before_parts)
    attention = (within + carried).astype(jnp.bfloat16).reshape(flat_shape)
    partial_output = lax.dot_general(
        attention, out_weight, (((1,), (1,)), ((), ())), preferred_element_type=jnp.float32
    ).astype(jnp.bfloat16)
    grad_scores = jnp.einsum(
        "cthe,cshe->chts", grad_blocks, value_blocks, preferred_element_type=jnp.float32
    )
    grad_weights = jnp.where(causal, factor * grad_scores, 0.0).astype(jnp.bfloat16)
    query_grad = jnp.einsum(
        "chts,cshd->cthd", grad_weights, key_blocks, preferred_element_type=jnp.float32
    )
    query_grad = query_grad + factor * state_product("cthe,chde->cthd", grad_blocks, before_parts)
    key_grad = jnp.einsum(
        "chts,cthd->cshd", grad_weights, query_blocks, preferred_element_type=jnp.float32
    )
    key_grad = key_grad + factor * state_product("cshe,chde->cshd", value_blocks, later_parts)
    value_grad = jnp.einsum(
        "chts,cthe->cshe", weights, grad_blocks, preferred_element_type=jnp.float32
    )
    value_grad = value_grad + factor * state_product("cshd,chde->cshe", key_blocks, later_parts)
    weight_partial = lax.dot_general(
        out_grad, attention, (((0,), (0,)), ((), ())), preferred_element_type=jnp.float32
    )
    core = lax.axis_index("c")
    halves = weight_partial.reshape(-1, 2, weight_partial.shape[0] // (2 * lax.axis_size("xy")), weight_partial.shape[1])
    kept = lax.dynamic_index_in_dim(halves, core, 1, keepdims=False)
    sent = lax.dynamic_index_in_dim(halves, 1 - core, 1, keepdims=False)
    kept = kept + lax.ppermute(sent, "c", [(0, 1), (1, 0)])
    kept, partial_output = lax.optimization_barrier((kept, partial_output))
    output = ring_scatter(partial_output, head_count_axis)
    weight_grad = lax.psum_scatter(
        kept.reshape(-1, weight_partial.shape[1]),
        "xy",
        scatter_dimension=0,
        tiled=True,
    ) * total_rows ** (-0.5)
    return (
        output,
        query_grad.astype(jnp.bfloat16).reshape(flat_shape),
        key_grad.astype(jnp.bfloat16).reshape(flat_shape),
        value_grad.astype(jnp.bfloat16).reshape(flat_shape),
        weight_grad,
    )


def solution(mesh):
    seq_count, head_count_axis = mesh.devices.shape
    split_mesh = Mesh(
        mesh.devices.reshape(seq_count // 2, 2, head_count_axis), ("xy", "c", "head")
    )

    def body(queries, key_rows, value_rows, out_weight, out_grad):
        return local(queries, key_rows, value_rows, out_weight, out_grad, seq_count, head_count_axis)

    return jax.shard_map(
        body,
        mesh=split_mesh,
        in_specs=(
            P(SEQ, "head"),
            P(SEQ, "head"),
            P(SEQ, "head"),
            P(None, "head"),
            P(SEQ, None),
        ),
        out_specs=(
            P(SEQ + ("head",), None),
            P(SEQ, "head"),
            P(SEQ, "head"),
            P(SEQ, "head"),
            P(SEQ, "head"),
        ),
        check_vma=False,
    )
```

```python
import jax
import jax.numpy as jnp
from jax import lax
from jax.sharding import Mesh
from jax.sharding import PartitionSpec as P

HD = 128
CH = 64
SEQ = ("xy", "c")


def swapped(block, count, distance):
    route = []
    for low in range(count):
        high = low | 1 << distance
        if high != low and high < count:
            route += [(low, high), (high, low)]
    return lax.ppermute(block, SEQ, route)


def split_state(state):
    upper = state.astype(jnp.bfloat16)
    lower = (state - upper.astype(jnp.float32)).astype(jnp.bfloat16)
    return (upper, lower)


def state_product(form, operand, parts):
    first = jnp.einsum(form, operand, parts[0], preferred_element_type=jnp.float32)
    return first + jnp.einsum(form, operand, parts[1], preferred_element_type=jnp.float32)


def halving_order(bits):
    if bits != 6:
        return list(range(bits))
    return [0, 1, 4, 2, 5, 3]


def halving_scatter(partial, count):
    bits = count.bit_length() - 1
    position = lax.axis_index(SEQ)
    cols = partial.shape[1]
    acc = partial.reshape((2,) * bits + (partial.shape[0] // count, cols))
    held = list(range(bits - 1, -1, -1))
    for bit in halving_order(bits):
        axis = held.index(bit)
        mine = position >> bit & 1
        lower = lax.index_in_dim(acc, 0, axis, keepdims=False)
        upper = lax.index_in_dim(acc, 1, axis, keepdims=False)
        kept = jnp.where(mine == 1, upper, lower)
        sent = jnp.where(mine == 1, lower, upper)
        route = [(i, i ^ 1 << bit) for i in range(count)]
        acc = kept + lax.ppermute(sent, SEQ, route)
        held.pop(axis)
    return acc.reshape(-1, cols)


def local(queries, key_rows, value_rows, out_weight, out_grad, seq_count, head_count_axis):
    local_rows = queries.shape[0]
    head_count = queries.shape[1] // HD
    blocks = local_rows // CH
    total_rows = local_rows * seq_count
    factor = (HD * total_rows) ** (-0.5)
    block_shape = (blocks, CH, head_count, HD)
    flat_shape = (local_rows, head_count * HD)
    query_blocks = queries.reshape(block_shape)
    key_blocks = key_rows.reshape(block_shape)
    value_blocks = value_rows.reshape(block_shape)
    causal = (jnp.arange(CH)[:, None] >= jnp.arange(CH)[None, :])[None, None]
    grad_rows = jnp.dot(out_grad, out_weight, preferred_element_type=jnp.float32).astype(
        jnp.bfloat16
    )
    grad_blocks = grad_rows.reshape(block_shape)
    key_value = jnp.einsum(
        "cshd,cshe->chde", key_blocks, value_blocks, preferred_element_type=jnp.float32
    )
    query_pairs = jnp.einsum(
        "cthd,cthe->chde", query_blocks, grad_blocks, preferred_element_type=jnp.float32
    )
    own_state = jnp.sum(key_value, 0)
    own_pairs = jnp.sum(query_pairs, 0)
    position = lax.axis_index(SEQ)
    level_count = seq_count.bit_length() - 1
    inflow = jnp.zeros_like(own_state)
    outflow = jnp.zeros_like(own_state)
    totals = jnp.stack([own_state, own_pairs])
    for level in range(level_count):
        other = swapped(totals.astype(jnp.bfloat16), seq_count, level).astype(jnp.float32)
        upper_half = position >> level & 1 == 1
        inflow = inflow + jnp.where(upper_half, other[0], 0.0)
        outflow = outflow + jnp.where(upper_half, 0.0, other[1])
        totals = totals + other
    before = inflow[None] + jnp.cumsum(key_value, 0) - key_value
    later_state = outflow[None] + own_pairs[None] - jnp.cumsum(query_pairs, 0)
    before_parts = split_state(before)
    later_parts = split_state(later_state)
    scores = jnp.einsum(
        "cthd,cshd->chts", query_blocks, key_blocks, preferred_element_type=jnp.float32
    )
    weights = jnp.where(causal, factor * scores, 0.0).astype(jnp.bfloat16)
    within = jnp.einsum(
        "chts,cshe->cthe", weights, value_blocks, preferred_element_type=jnp.float32
    )
    carried = factor * state_product("cthd,chde->cthe", query_blocks, before_parts)
    attention = (within + carried).astype(jnp.bfloat16).reshape(flat_shape)
    partial_output = lax.dot_general(
        attention, out_weight, (((1,), (1,)), ((), ())), preferred_element_type=jnp.float32
    ).astype(jnp.bfloat16)
    grad_scores = jnp.einsum(
        "cthe,cshe->chts", grad_blocks, value_blocks, preferred_element_type=jnp.float32
    )
    grad_weights = jnp.where(causal, factor * grad_scores, 0.0).astype(jnp.bfloat16)
    query_grad = jnp.einsum(
        "chts,cshd->cthd", grad_weights, key_blocks, preferred_element_type=jnp.float32
    )
    query_grad = query_grad + factor * state_product("cthe,chde->cthd", grad_blocks, before_parts)
    key_grad = jnp.einsum(
        "chts,cthd->cshd", grad_weights, query_blocks, preferred_element_type=jnp.float32
    )
    key_grad = key_grad + factor * state_product("cshe,chde->cshd", value_blocks, later_parts)
    value_grad = jnp.einsum(
        "chts,cthe->cshe", weights, grad_blocks, preferred_element_type=jnp.float32
    )
    value_grad = value_grad + factor * state_product("cshd,chde->cshe", key_blocks, later_parts)
    weight_partial = lax.dot_general(
        out_grad, attention, (((0,), (0,)), ((), ())), preferred_element_type=jnp.float32
    )
    partial_output, weight_partial = lax.optimization_barrier((partial_output, weight_partial))
    output = lax.psum_scatter(partial_output, "head", scatter_dimension=0, tiled=True)
    weight_grad = halving_scatter(weight_partial, seq_count) * total_rows ** (-0.5)
    return (
        output,
        query_grad.astype(jnp.bfloat16).reshape(flat_shape),
        key_grad.astype(jnp.bfloat16).reshape(flat_shape),
        value_grad.astype(jnp.bfloat16).reshape(flat_shape),
        weight_grad,
    )


def solution(mesh):
    seq_count, head_count_axis = mesh.devices.shape
    split_mesh = Mesh(
        mesh.devices.reshape(seq_count // 2, 2, head_count_axis), ("xy", "c", "head")
    )

    def body(queries, key_rows, value_rows, out_weight, out_grad):
        return local(queries, key_rows, value_rows, out_weight, out_grad, seq_count, head_count_axis)

    return jax.shard_map(
        body,
        mesh=split_mesh,
        in_specs=(
            P(SEQ, "head"),
            P(SEQ, "head"),
            P(SEQ, "head"),
            P(None, "head"),
            P(SEQ, None),
        ),
        out_specs=(
            P(SEQ + ("head",), None),
            P(SEQ, "head"),
            P(SEQ, "head"),
            P(SEQ, "head"),
            P(SEQ, "head"),
        ),
        check_vma=False,
    )
```

```python
import jax
import jax.numpy as jnp
from jax import lax
from jax.sharding import Mesh
from jax.sharding import PartitionSpec as P

HD = 128
CH = 64
SEQ = ("xy", "c")


def swapped(block, count, distance):
    route = []
    for low in range(count):
        high = low | 1 << distance
        if high != low and high < count:
            route += [(low, high), (high, low)]
    return lax.ppermute(block, SEQ, route)


def split_state(state):
    upper = state.astype(jnp.bfloat16)
    lower = (state - upper.astype(jnp.float32)).astype(jnp.bfloat16)
    return (upper, lower)


def state_product(form, operand, parts):
    first = jnp.einsum(form, operand, parts[0], preferred_element_type=jnp.float32)
    return first + jnp.einsum(form, operand, parts[1], preferred_element_type=jnp.float32)


def halving_order(bits):
    if bits != 6:
        return list(range(bits))
    return [0, 1, 4, 2, 5, 3]


def halving_scatter(partial, count):
    bits = count.bit_length() - 1
    position = lax.axis_index(SEQ)
    cols = partial.shape[1]
    acc = partial.reshape((2,) * bits + (partial.shape[0] // count, cols))
    held = list(range(bits - 1, -1, -1))
    for bit in halving_order(bits):
        axis = held.index(bit)
        mine = position >> bit & 1
        lower = lax.index_in_dim(acc, 0, axis, keepdims=False)
        upper = lax.index_in_dim(acc, 1, axis, keepdims=False)
        kept = jnp.where(mine == 1, upper, lower)
        sent = jnp.where(mine == 1, lower, upper)
        route = [(i, i ^ 1 << bit) for i in range(count)]
        acc = kept + lax.ppermute(sent, SEQ, route)
        held.pop(axis)
    return acc.reshape(-1, cols)


def grid_scatter(partial, x_count, y_count):
    count = x_count * y_count * 2
    cols = partial.shape[1]
    position = lax.axis_index(SEQ)
    core = position % 2
    y = position // 2 % y_count
    x = position // (2 * y_count)
    index = lambda a, b, c: a * 2 * y_count + b % y_count * 2 + c
    acc = partial.reshape(x_count, y_count, 2, partial.shape[0] // count, cols)
    kept = lax.dynamic_index_in_dim(acc, core, 2, keepdims=False)
    sent = lax.dynamic_index_in_dim(acc, 1 - core, 2, keepdims=False)
    acc = kept + lax.ppermute(sent, SEQ, [(i, i ^ 1) for i in range(count)])
    acc = jnp.where(core == 1, jnp.roll(acc, -1, axis=1), acc)
    acc = acc.reshape(x_count, y_count // 2, 2, acc.shape[2], cols)
    label = (y - core) % y_count
    odd = label % 2
    route = []
    for a in range(x_count):
        for b in range(y_count):
            for c in range(2):
                other = ((b - c) % y_count ^ 1) + c
                route.append((index(a, b, c), index(a, other, c)))
    kept = lax.dynamic_index_in_dim(acc, odd, 2, keepdims=False)
    sent = lax.dynamic_index_in_dim(acc, 1 - odd, 2, keepdims=False)
    acc = kept + lax.ppermute(sent, SEQ, route)
    total = lax.dynamic_index_in_dim(acc, x, 0, keepdims=False)
    for shift in range(1, x_count):
        piece = lax.dynamic_index_in_dim(acc, (x + shift) % x_count, 0, keepdims=False)
        route = [(index(a, b, c), index((a + shift) % x_count, b, c))
                 for a in range(x_count) for b in range(y_count) for c in range(2)]
        total = total + lax.ppermute(piece, SEQ, route)
    acc = total
    quarter = label // 2
    groups = y_count // 2
    total = lax.dynamic_index_in_dim(acc, quarter, 0, keepdims=False)
    for shift in range(1, groups):
        piece = lax.dynamic_index_in_dim(acc, (quarter + shift) % groups, 0, keepdims=False)
        route = [(index(a, b, c), index(a, b + 2 * shift, c))
                 for a in range(x_count) for b in range(y_count) for c in range(2)]
        total = total + lax.ppermute(piece, SEQ, route)
    return total


def local(queries, key_rows, value_rows, out_weight, out_grad, seq_count, head_count_axis):
    local_rows = queries.shape[0]
    head_count = queries.shape[1] // HD
    blocks = local_rows // CH
    total_rows = local_rows * seq_count
    factor = (HD * total_rows) ** (-0.5)
    block_shape = (blocks, CH, head_count, HD)
    flat_shape = (local_rows, head_count * HD)
    query_blocks = queries.reshape(block_shape)
    key_blocks = key_rows.reshape(block_shape)
    value_blocks = value_rows.reshape(block_shape)
    causal = (jnp.arange(CH)[:, None] >= jnp.arange(CH)[None, :])[None, None]
    grad_rows = jnp.dot(out_grad, out_weight, preferred_element_type=jnp.float32).astype(
        jnp.bfloat16
    )
    grad_blocks = grad_rows.reshape(block_shape)
    key_value = jnp.einsum(
        "cshd,cshe->chde", key_blocks, value_blocks, preferred_element_type=jnp.float32
    )
    query_pairs = jnp.einsum(
        "cthd,cthe->chde", query_blocks, grad_blocks, preferred_element_type=jnp.float32
    )
    own_state = jnp.sum(key_value, 0)
    own_pairs = jnp.sum(query_pairs, 0)
    position = lax.axis_index(SEQ)
    level_count = seq_count.bit_length() - 1
    inflow = jnp.zeros_like(own_state)
    outflow = jnp.zeros_like(own_state)
    totals = jnp.stack([own_state, own_pairs])
    for level in range(level_count):
        other = swapped(totals.astype(jnp.bfloat16), seq_count, level).astype(jnp.float32)
        upper_half = position >> level & 1 == 1
        inflow = inflow + jnp.where(upper_half, other[0], 0.0)
        outflow = outflow + jnp.where(upper_half, 0.0, other[1])
        totals = totals + other
    before = inflow[None] + jnp.cumsum(key_value, 0) - key_value
    later_state = outflow[None] + own_pairs[None] - jnp.cumsum(query_pairs, 0)
    before_parts = split_state(before)
    later_parts = split_state(later_state)
    scores = jnp.einsum(
        "cthd,cshd->chts", query_blocks, key_blocks, preferred_element_type=jnp.float32
    )
    weights = jnp.where(causal, factor * scores, 0.0).astype(jnp.bfloat16)
    within = jnp.einsum(
        "chts,cshe->cthe", weights, value_blocks, preferred_element_type=jnp.float32
    )
    carried = factor * state_product("cthd,chde->cthe", query_blocks, before_parts)
    attention = (within + carried).astype(jnp.bfloat16).reshape(flat_shape)
    partial_output = lax.dot_general(
        attention, out_weight, (((1,), (1,)), ((), ())), preferred_element_type=jnp.float32
    ).astype(jnp.bfloat16)
    grad_scores = jnp.einsum(
        "cthe,cshe->chts", grad_blocks, value_blocks, preferred_element_type=jnp.float32
    )
    grad_weights = jnp.where(causal, factor * grad_scores, 0.0).astype(jnp.bfloat16)
    query_grad = jnp.einsum(
        "chts,cshd->cthd", grad_weights, key_blocks, preferred_element_type=jnp.float32
    )
    query_grad = query_grad + factor * state_product("cthe,chde->cthd", grad_blocks, before_parts)
    key_grad = jnp.einsum(
        "chts,cthd->cshd", grad_weights, query_blocks, preferred_element_type=jnp.float32
    )
    key_grad = key_grad + factor * state_product("cshe,chde->cshd", value_blocks, later_parts)
    value_grad = jnp.einsum(
        "chts,cthe->cshe", weights, grad_blocks, preferred_element_type=jnp.float32
    )
    value_grad = value_grad + factor * state_product("cshd,chde->cshe", key_blocks, later_parts)
    weight_partial = lax.dot_general(
        out_grad, attention, (((0,), (0,)), ((), ())), preferred_element_type=jnp.float32
    )
    partial_output, weight_partial = lax.optimization_barrier((partial_output, weight_partial))
    output = lax.psum_scatter(partial_output, "head", scatter_dimension=0, tiled=True)
    if seq_count == 64:
        weight_grad = grid_scatter(weight_partial, 4, 8)
    else:
        weight_grad = halving_scatter(weight_partial, seq_count)
    weight_grad = weight_grad * total_rows ** (-0.5)
    return (
        output,
        query_grad.astype(jnp.bfloat16).reshape(flat_shape),
        key_grad.astype(jnp.bfloat16).reshape(flat_shape),
        value_grad.astype(jnp.bfloat16).reshape(flat_shape),
        weight_grad,
    )


def solution(mesh):
    seq_count, head_count_axis = mesh.devices.shape
    split_mesh = Mesh(
        mesh.devices.reshape(seq_count // 2, 2, head_count_axis), ("xy", "c", "head")
    )

    def body(queries, key_rows, value_rows, out_weight, out_grad):
        return local(queries, key_rows, value_rows, out_weight, out_grad, seq_count, head_count_axis)

    return jax.shard_map(
        body,
        mesh=split_mesh,
        in_specs=(
            P(SEQ, "head"),
            P(SEQ, "head"),
            P(SEQ, "head"),
            P(None, "head"),
            P(SEQ, None),
        ),
        out_specs=(
            P(SEQ + ("head",), None),
            P(SEQ, "head"),
            P(SEQ, "head"),
            P(SEQ, "head"),
            P(SEQ, "head"),
        ),
        check_vma=False,
    )
```

```python
import jax
import jax.numpy as jnp
from jax import lax
from jax.sharding import Mesh
from jax.sharding import PartitionSpec as P

HD = 128
CH = 64
SEQ = ("xy", "c")


def swapped(block, count, distance):
    route = []
    for low in range(count):
        high = low | 1 << distance
        if high != low and high < count:
            route += [(low, high), (high, low)]
    return lax.ppermute(block, SEQ, route)


def split_state(state):
    upper = state.astype(jnp.bfloat16)
    lower = (state - upper.astype(jnp.float32)).astype(jnp.bfloat16)
    return (upper, lower)


def state_product(form, operand, parts):
    first = jnp.einsum(form, operand, parts[0], preferred_element_type=jnp.float32)
    return first + jnp.einsum(form, operand, parts[1], preferred_element_type=jnp.float32)


def halving_order(bits):
    if bits != 6:
        return list(range(bits))
    return [0, 1, 4, 2, 5, 3]


def halving_scatter(partial, count):
    bits = count.bit_length() - 1
    position = lax.axis_index(SEQ)
    cols = partial.shape[1]
    acc = partial.reshape((2,) * bits + (partial.shape[0] // count, cols))
    held = list(range(bits - 1, -1, -1))
    for bit in halving_order(bits):
        axis = held.index(bit)
        mine = position >> bit & 1
        lower = lax.index_in_dim(acc, 0, axis, keepdims=False)
        upper = lax.index_in_dim(acc, 1, axis, keepdims=False)
        kept = jnp.where(mine == 1, upper, lower)
        sent = jnp.where(mine == 1, lower, upper)
        route = [(i, i ^ 1 << bit) for i in range(count)]
        acc = kept + lax.ppermute(sent, SEQ, route)
        held.pop(axis)
    return acc.reshape(-1, cols)


def wire(block, route):
    return lax.ppermute(block.astype(jnp.bfloat16), SEQ, route).astype(jnp.float32)


def grid_scatter(partial, x_count, y_count):
    count = x_count * y_count * 2
    cols = partial.shape[1]
    position = lax.axis_index(SEQ)
    core = position % 2
    y = position // 2 % y_count
    x = position // (2 * y_count)
    index = lambda a, b, c: a * 2 * y_count + b % y_count * 2 + c
    acc = partial.reshape(x_count, y_count, 2, partial.shape[0] // count, cols)
    kept = lax.dynamic_index_in_dim(acc, core, 2, keepdims=False)
    sent = lax.dynamic_index_in_dim(acc, 1 - core, 2, keepdims=False)
    acc = kept + lax.ppermute(sent, SEQ, [(i, i ^ 1) for i in range(count)])
    acc = jnp.where(core == 1, jnp.roll(acc, -1, axis=1), acc)
    acc = acc.reshape(x_count, y_count // 2, 2, acc.shape[2], cols)
    label = (y - core) % y_count
    odd = label % 2
    route = []
    for a in range(x_count):
        for b in range(y_count):
            for c in range(2):
                other = ((b - c) % y_count ^ 1) + c
                route.append((index(a, b, c), index(a, other, c)))
    kept = lax.dynamic_index_in_dim(acc, odd, 2, keepdims=False)
    sent = lax.dynamic_index_in_dim(acc, 1 - odd, 2, keepdims=False)
    acc = kept + wire(sent, route)
    total = lax.dynamic_index_in_dim(acc, x, 0, keepdims=False)
    for shift in range(1, x_count):
        piece = lax.dynamic_index_in_dim(acc, (x + shift) % x_count, 0, keepdims=False)
        route = [(index(a, b, c), index((a + shift) % x_count, b, c))
                 for a in range(x_count) for b in range(y_count) for c in range(2)]
        total = total + wire(piece, route)
    acc = total
    quarter = label // 2
    groups = y_count // 2
    total = lax.dynamic_index_in_dim(acc, quarter, 0, keepdims=False)
    for shift in range(1, groups):
        piece = lax.dynamic_index_in_dim(acc, (quarter + shift) % groups, 0, keepdims=False)
        route = [(index(a, b, c), index(a, b + 2 * shift, c))
                 for a in range(x_count) for b in range(y_count) for c in range(2)]
        total = total + wire(piece, route)
    return total


def local(queries, key_rows, value_rows, out_weight, out_grad, seq_count, head_count_axis):
    local_rows = queries.shape[0]
    head_count = queries.shape[1] // HD
    blocks = local_rows // CH
    total_rows = local_rows * seq_count
    factor = (HD * total_rows) ** (-0.5)
    block_shape = (blocks, CH, head_count, HD)
    flat_shape = (local_rows, head_count * HD)
    query_blocks = queries.reshape(block_shape)
    key_blocks = key_rows.reshape(block_shape)
    value_blocks = value_rows.reshape(block_shape)
    causal = (jnp.arange(CH)[:, None] >= jnp.arange(CH)[None, :])[None, None]
    grad_rows = jnp.dot(out_grad, out_weight, preferred_element_type=jnp.float32).astype(
        jnp.bfloat16
    )
    grad_blocks = grad_rows.reshape(block_shape)
    key_value = jnp.einsum(
        "cshd,cshe->chde", key_blocks, value_blocks, preferred_element_type=jnp.float32
    )
    query_pairs = jnp.einsum(
        "cthd,cthe->chde", query_blocks, grad_blocks, preferred_element_type=jnp.float32
    )
    own_state = jnp.stack([
        lax.dot_general(
            key_rows[:, h * HD:(h + 1) * HD], value_rows[:, h * HD:(h + 1) * HD],
            (((0,), (0,)), ((), ())), preferred_element_type=jnp.float32,
        )
        for h in range(head_count)
    ])
    own_pairs = jnp.stack([
        lax.dot_general(
            queries[:, h * HD:(h + 1) * HD], grad_rows[:, h * HD:(h + 1) * HD],
            (((0,), (0,)), ((), ())), preferred_element_type=jnp.float32,
        )
        for h in range(head_count)
    ])
    position = lax.axis_index(SEQ)
    level_count = seq_count.bit_length() - 1
    inflow = jnp.zeros_like(own_state)
    outflow = jnp.zeros_like(own_state)
    totals = jnp.stack([own_state, own_pairs])
    for level in range(level_count):
        other = swapped(totals.astype(jnp.bfloat16), seq_count, level).astype(jnp.float32)
        upper_half = position >> level & 1 == 1
        inflow = inflow + jnp.where(upper_half, other[0], 0.0)
        outflow = outflow + jnp.where(upper_half, 0.0, other[1])
        totals = totals + other
    before = inflow[None] + jnp.cumsum(key_value, 0) - key_value
    later_state = outflow[None] + own_pairs[None] - jnp.cumsum(query_pairs, 0)
    before_parts = split_state(before)
    later_parts = split_state(later_state)
    scores = jnp.einsum(
        "cthd,cshd->chts", query_blocks, key_blocks, preferred_element_type=jnp.float32
    )
    weights = jnp.where(causal, factor * scores, 0.0).astype(jnp.bfloat16)
    within = jnp.einsum(
        "chts,cshe->cthe", weights, value_blocks, preferred_element_type=jnp.float32
    )
    carried = factor * state_product("cthd,chde->cthe", query_blocks, before_parts)
    attention = (within + carried).astype(jnp.bfloat16).reshape(flat_shape)
    partial_output = lax.dot_general(
        attention, out_weight, (((1,), (1,)), ((), ())), preferred_element_type=jnp.float32
    ).astype(jnp.bfloat16)
    grad_scores = jnp.einsum(
        "cthe,cshe->chts", grad_blocks, value_blocks, preferred_element_type=jnp.float32
    )
    grad_weights = jnp.where(causal, factor * grad_scores, 0.0).astype(jnp.bfloat16)
    query_grad = jnp.einsum(
        "chts,cshd->cthd", grad_weights, key_blocks, preferred_element_type=jnp.float32
    )
    query_grad = query_grad + factor * state_product("cthe,chde->cthd", grad_blocks, before_parts)
    key_grad = jnp.einsum(
        "chts,cthd->cshd", grad_weights, query_blocks, preferred_element_type=jnp.float32
    )
    key_grad = key_grad + factor * state_product("cshe,chde->cshd", value_blocks, later_parts)
    value_grad = jnp.einsum(
        "chts,cthe->cshe", weights, grad_blocks, preferred_element_type=jnp.float32
    )
    value_grad = value_grad + factor * state_product("cshd,chde->cshe", key_blocks, later_parts)
    partial_output, attention = lax.optimization_barrier((partial_output, attention))
    output = lax.psum_scatter(partial_output, "head", scatter_dimension=0, tiled=True)
    weight_partial = lax.dot_general(
        out_grad, attention, (((0,), (0,)), ((), ())), preferred_element_type=jnp.float32
    )
    if seq_count == 64:
        weight_grad = grid_scatter(weight_partial, 4, 8)
    else:
        weight_grad = halving_scatter(weight_partial, seq_count)
    weight_grad = weight_grad * total_rows ** (-0.5)
    return (
        output,
        query_grad.astype(jnp.bfloat16).reshape(flat_shape),
        key_grad.astype(jnp.bfloat16).reshape(flat_shape),
        value_grad.astype(jnp.bfloat16).reshape(flat_shape),
        weight_grad,
    )


def solution(mesh):
    seq_count, head_count_axis = mesh.devices.shape
    split_mesh = Mesh(
        mesh.devices.reshape(seq_count // 2, 2, head_count_axis), ("xy", "c", "head")
    )

    def body(queries, key_rows, value_rows, out_weight, out_grad):
        return local(queries, key_rows, value_rows, out_weight, out_grad, seq_count, head_count_axis)

    return jax.shard_map(
        body,
        mesh=split_mesh,
        in_specs=(
            P(SEQ, "head"),
            P(SEQ, "head"),
            P(SEQ, "head"),
            P(None, "head"),
            P(SEQ, None),
        ),
        out_specs=(
            P(SEQ + ("head",), None),
            P(SEQ, "head"),
            P(SEQ, "head"),
            P(SEQ, "head"),
            P(SEQ, "head"),
        ),
        check_vma=False,
    )
```

```python
import jax
import jax.numpy as jnp
from jax import lax
from jax.sharding import Mesh
from jax.sharding import PartitionSpec as P

HD = 128
CH = 64
SEQ = ("xy", "c")


def swapped(block, count, distance):
    route = []
    for low in range(count):
        high = low | 1 << distance
        if high != low and high < count:
            route += [(low, high), (high, low)]
    return lax.ppermute(block, SEQ, route)


def split_state(state):
    upper = state.astype(jnp.bfloat16)
    lower = (state - upper.astype(jnp.float32)).astype(jnp.bfloat16)
    return (upper, lower)


def state_product(form, operand, parts):
    first = jnp.einsum(form, operand, parts[0], preferred_element_type=jnp.float32)
    return first + jnp.einsum(form, operand, parts[1], preferred_element_type=jnp.float32)


def halving_order(bits):
    if bits != 6:
        return list(range(bits))
    return [0, 1, 4, 2, 5, 3]


def halving_scatter(partial, count):
    bits = count.bit_length() - 1
    position = lax.axis_index(SEQ)
    cols = partial.shape[1]
    acc = partial.reshape((2,) * bits + (partial.shape[0] // count, cols))
    held = list(range(bits - 1, -1, -1))
    for bit in halving_order(bits):
        axis = held.index(bit)
        mine = position >> bit & 1
        lower = lax.index_in_dim(acc, 0, axis, keepdims=False)
        upper = lax.index_in_dim(acc, 1, axis, keepdims=False)
        kept = jnp.where(mine == 1, upper, lower)
        sent = jnp.where(mine == 1, lower, upper)
        route = [(i, i ^ 1 << bit) for i in range(count)]
        acc = kept + lax.ppermute(sent, SEQ, route)
        held.pop(axis)
    return acc.reshape(-1, cols)


def wire(block, route):
    return lax.ppermute(block.astype(jnp.bfloat16), SEQ, route).astype(jnp.float32)


def grid_scatter(partial, x_count, y_count, ride):
    count = x_count * y_count * 2
    cols = partial.shape[1]
    position = lax.axis_index(SEQ)
    core = position % 2
    y = position // 2 % y_count
    x = position // (2 * y_count)
    index = lambda a, b, c: a * 2 * y_count + b % y_count * 2 + c
    acc = partial.reshape(x_count, y_count, 2, partial.shape[0] // count, cols)
    kept = lax.dynamic_index_in_dim(acc, core, 2, keepdims=False)
    sent = lax.dynamic_index_in_dim(acc, 1 - core, 2, keepdims=False)
    acc = kept + lax.ppermute(sent, SEQ, [(i, i ^ 1) for i in range(count)])
    acc, ride = lax.optimization_barrier((acc, ride))
    acc = jnp.where(core == 1, jnp.roll(acc, -1, axis=1), acc)
    acc = acc.reshape(x_count, y_count // 2, 2, acc.shape[2], cols)
    label = (y - core) % y_count
    odd = label % 2
    route = []
    for a in range(x_count):
        for b in range(y_count):
            for c in range(2):
                other = ((b - c) % y_count ^ 1) + c
                route.append((index(a, b, c), index(a, other, c)))
    kept = lax.dynamic_index_in_dim(acc, odd, 2, keepdims=False)
    sent = lax.dynamic_index_in_dim(acc, 1 - odd, 2, keepdims=False)
    acc = kept + wire(sent, route)
    total = lax.dynamic_index_in_dim(acc, x, 0, keepdims=False)
    for shift in range(1, x_count):
        piece = lax.dynamic_index_in_dim(acc, (x + shift) % x_count, 0, keepdims=False)
        route = [(index(a, b, c), index((a + shift) % x_count, b, c))
                 for a in range(x_count) for b in range(y_count) for c in range(2)]
        total = total + wire(piece, route)
    acc = total
    quarter = label // 2
    groups = y_count // 2
    total = lax.dynamic_index_in_dim(acc, quarter, 0, keepdims=False)
    for shift in range(1, groups):
        piece = lax.dynamic_index_in_dim(acc, (quarter + shift) % groups, 0, keepdims=False)
        route = [(index(a, b, c), index(a, b + 2 * shift, c))
                 for a in range(x_count) for b in range(y_count) for c in range(2)]
        total = total + wire(piece, route)
    return total, ride


def local(queries, key_rows, value_rows, out_weight, out_grad, seq_count, head_count_axis):
    local_rows = queries.shape[0]
    head_count = queries.shape[1] // HD
    blocks = local_rows // CH
    total_rows = local_rows * seq_count
    factor = (HD * total_rows) ** (-0.5)
    block_shape = (blocks, CH, head_count, HD)
    flat_shape = (local_rows, head_count * HD)
    query_blocks = queries.reshape(block_shape)
    key_blocks = key_rows.reshape(block_shape)
    value_blocks = value_rows.reshape(block_shape)
    causal = (jnp.arange(CH)[:, None] >= jnp.arange(CH)[None, :])[None, None]
    grad_rows = jnp.dot(out_grad, out_weight, preferred_element_type=jnp.float32).astype(
        jnp.bfloat16
    )
    grad_blocks = grad_rows.reshape(block_shape)
    key_value = jnp.einsum(
        "cshd,cshe->chde", key_blocks, value_blocks, preferred_element_type=jnp.float32
    )
    query_pairs = jnp.einsum(
        "cthd,cthe->chde", query_blocks, grad_blocks, preferred_element_type=jnp.float32
    )
    own_state = jnp.stack([
        lax.dot_general(
            key_rows[:, h * HD:(h + 1) * HD], value_rows[:, h * HD:(h + 1) * HD],
            (((0,), (0,)), ((), ())), preferred_element_type=jnp.float32,
        )
        for h in range(head_count)
    ])
    own_pairs = jnp.stack([
        lax.dot_general(
            queries[:, h * HD:(h + 1) * HD], grad_rows[:, h * HD:(h + 1) * HD],
            (((0,), (0,)), ((), ())), preferred_element_type=jnp.float32,
        )
        for h in range(head_count)
    ])
    position = lax.axis_index(SEQ)
    level_count = seq_count.bit_length() - 1
    inflow = jnp.zeros_like(own_state)
    outflow = jnp.zeros_like(own_state)
    totals = jnp.stack([own_state, own_pairs])
    for level in range(level_count):
        other = swapped(totals.astype(jnp.bfloat16), seq_count, level).astype(jnp.float32)
        upper_half = position >> level & 1 == 1
        inflow = inflow + jnp.where(upper_half, other[0], 0.0)
        outflow = outflow + jnp.where(upper_half, 0.0, other[1])
        totals = totals + other
    before = inflow[None] + jnp.cumsum(key_value, 0) - key_value
    later_state = outflow[None] + own_pairs[None] - jnp.cumsum(query_pairs, 0)
    before_parts = split_state(before)
    later_parts = split_state(later_state)
    scores = jnp.einsum(
        "cthd,cshd->chts", query_blocks, key_blocks, preferred_element_type=jnp.float32
    )
    weights = jnp.where(causal, factor * scores, 0.0).astype(jnp.bfloat16)
    within = jnp.einsum(
        "chts,cshe->cthe", weights, value_blocks, preferred_element_type=jnp.float32
    )
    carried = factor * state_product("cthd,chde->cthe", query_blocks, before_parts)
    attention = (within + carried).astype(jnp.bfloat16).reshape(flat_shape)
    partial_output = lax.dot_general(
        attention, out_weight, (((1,), (1,)), ((), ())), preferred_element_type=jnp.float32
    ).astype(jnp.bfloat16)
    partial_output, attention = lax.optimization_barrier((partial_output, attention))
    output = lax.psum_scatter(partial_output, "head", scatter_dimension=0, tiled=True)
    weight_partial = lax.dot_general(
        out_grad, attention, (((0,), (0,)), ((), ())), preferred_element_type=jnp.float32
    )
    if seq_count == 64:
        weight_grad, (before_parts, later_parts) = grid_scatter(
            weight_partial, 4, 8, (before_parts, later_parts)
        )
    else:
        weight_grad = halving_scatter(weight_partial, seq_count)
    grad_scores = jnp.einsum(
        "cthe,cshe->chts", grad_blocks, value_blocks, preferred_element_type=jnp.float32
    )
    grad_weights = jnp.where(causal, factor * grad_scores, 0.0).astype(jnp.bfloat16)
    query_grad = jnp.einsum(
        "chts,cshd->cthd", grad_weights, key_blocks, preferred_element_type=jnp.float32
    )
    query_grad = query_grad + factor * state_product("cthe,chde->cthd", grad_blocks, before_parts)
    key_grad = jnp.einsum(
        "chts,cthd->cshd", grad_weights, query_blocks, preferred_element_type=jnp.float32
    )
    key_grad = key_grad + factor * state_product("cshe,chde->cshd", value_blocks, later_parts)
    value_grad = jnp.einsum(
        "chts,cthe->cshe", weights, grad_blocks, preferred_element_type=jnp.float32
    )
    value_grad = value_grad + factor * state_product("cshd,chde->cshe", key_blocks, later_parts)
    weight_grad = weight_grad * total_rows ** (-0.5)
    return (
        output,
        query_grad.astype(jnp.bfloat16).reshape(flat_shape),
        key_grad.astype(jnp.bfloat16).reshape(flat_shape),
        value_grad.astype(jnp.bfloat16).reshape(flat_shape),
        weight_grad,
    )


def solution(mesh):
    seq_count, head_count_axis = mesh.devices.shape
    split_mesh = Mesh(
        mesh.devices.reshape(seq_count // 2, 2, head_count_axis), ("xy", "c", "head")
    )

    def body(queries, key_rows, value_rows, out_weight, out_grad):
        return local(queries, key_rows, value_rows, out_weight, out_grad, seq_count, head_count_axis)

    return jax.shard_map(
        body,
        mesh=split_mesh,
        in_specs=(
            P(SEQ, "head"),
            P(SEQ, "head"),
            P(SEQ, "head"),
            P(None, "head"),
            P(SEQ, None),
        ),
        out_specs=(
            P(SEQ + ("head",), None),
            P(SEQ, "head"),
            P(SEQ, "head"),
            P(SEQ, "head"),
            P(SEQ, "head"),
        ),
        check_vma=False,
    )
```

```python
import jax
import jax.numpy as jnp
from jax import lax
from jax.sharding import Mesh
from jax.sharding import PartitionSpec as P

HD = 128
CH = 64
SEQ = ("xy", "c")


def swapped(block, count, distance):
    route = []
    for low in range(count):
        high = low | 1 << distance
        if high != low and high < count:
            route += [(low, high), (high, low)]
    return lax.ppermute(block, SEQ, route)


def split_state(state):
    upper = state.astype(jnp.bfloat16)
    lower = (state - upper.astype(jnp.float32)).astype(jnp.bfloat16)
    return (upper, lower)


def state_product(form, operand, parts):
    first = jnp.einsum(form, operand, parts[0], preferred_element_type=jnp.float32)
    return first + jnp.einsum(form, operand, parts[1], preferred_element_type=jnp.float32)


def halving_order(bits):
    if bits != 6:
        return list(range(bits))
    return [0, 1, 4, 2, 5, 3]


def halving_scatter(partial, count):
    bits = count.bit_length() - 1
    position = lax.axis_index(SEQ)
    cols = partial.shape[1]
    acc = partial.reshape((2,) * bits + (partial.shape[0] // count, cols))
    held = list(range(bits - 1, -1, -1))
    for bit in halving_order(bits):
        axis = held.index(bit)
        mine = position >> bit & 1
        lower = lax.index_in_dim(acc, 0, axis, keepdims=False)
        upper = lax.index_in_dim(acc, 1, axis, keepdims=False)
        kept = jnp.where(mine == 1, upper, lower)
        sent = jnp.where(mine == 1, lower, upper)
        route = [(i, i ^ 1 << bit) for i in range(count)]
        acc = kept + lax.ppermute(sent, SEQ, route)
        held.pop(axis)
    return acc.reshape(-1, cols)


def wire(block, route):
    return lax.ppermute(block.astype(jnp.bfloat16), SEQ, route).astype(jnp.float32)


def grid_scatter(partial, x_count, y_count, ride):
    count = x_count * y_count * 2
    cols = partial.shape[1]
    position = lax.axis_index(SEQ)
    core = position % 2
    y = position // 2 % y_count
    x = position // (2 * y_count)
    index = lambda a, b, c: a * 2 * y_count + b % y_count * 2 + c
    acc = partial.reshape(x_count, y_count, 2, partial.shape[0] // count, cols)
    kept = lax.dynamic_index_in_dim(acc, core, 2, keepdims=False)
    sent = lax.dynamic_index_in_dim(acc, 1 - core, 2, keepdims=False)
    acc = kept + lax.ppermute(sent, SEQ, [(i, i ^ 1) for i in range(count)])
    acc, ride = lax.optimization_barrier((acc, ride))
    acc = jnp.where(core == 1, jnp.roll(acc, -1, axis=1), acc)
    acc = acc.reshape(x_count, y_count // 2, 2, acc.shape[2], cols)
    label = (y - core) % y_count
    odd = label % 2
    route = []
    for a in range(x_count):
        for b in range(y_count):
            for c in range(2):
                other = ((b - c) % y_count ^ 1) + c
                route.append((index(a, b, c), index(a, other, c)))
    kept = lax.dynamic_index_in_dim(acc, odd, 2, keepdims=False)
    sent = lax.dynamic_index_in_dim(acc, 1 - odd, 2, keepdims=False)
    acc = kept + wire(sent, route)
    total = lax.dynamic_index_in_dim(acc, x, 0, keepdims=False)
    for shift in range(1, x_count):
        piece = lax.dynamic_index_in_dim(acc, (x + shift) % x_count, 0, keepdims=False)
        route = [(index(a, b, c), index((a + shift) % x_count, b, c))
                 for a in range(x_count) for b in range(y_count) for c in range(2)]
        total = total + wire(piece, route)
    acc = total
    quarter = label // 2
    groups = y_count // 2
    total = lax.dynamic_index_in_dim(acc, quarter, 0, keepdims=False)
    for shift in range(1, groups):
        piece = lax.dynamic_index_in_dim(acc, (quarter + shift) % groups, 0, keepdims=False)
        route = [(index(a, b, c), index(a, b + 2 * shift, c))
                 for a in range(x_count) for b in range(y_count) for c in range(2)]
        total = total + wire(piece, route)
    return total, ride


def local(queries, key_rows, value_rows, out_weight, out_grad, seq_count, head_count_axis):
    local_rows = queries.shape[0]
    head_count = queries.shape[1] // HD
    blocks = local_rows // CH
    total_rows = local_rows * seq_count
    factor = (HD * total_rows) ** (-0.5)
    block_shape = (blocks, CH, head_count, HD)
    flat_shape = (local_rows, head_count * HD)
    query_blocks = queries.reshape(block_shape)
    key_blocks = key_rows.reshape(block_shape)
    value_blocks = value_rows.reshape(block_shape)
    causal = (jnp.arange(CH)[:, None] >= jnp.arange(CH)[None, :])[None, None]
    grad_rows = jnp.dot(out_grad, out_weight, preferred_element_type=jnp.float32).astype(
        jnp.bfloat16
    )
    grad_blocks = grad_rows.reshape(block_shape)
    key_value = jnp.einsum(
        "cshd,cshe->chde", key_blocks, value_blocks, preferred_element_type=jnp.float32
    )
    query_pairs = jnp.einsum(
        "cthd,cthe->chde", query_blocks, grad_blocks, preferred_element_type=jnp.float32
    )
    own_state = jnp.stack([
        lax.dot_general(
            key_rows[:, h * HD:(h + 1) * HD], value_rows[:, h * HD:(h + 1) * HD],
            (((0,), (0,)), ((), ())), preferred_element_type=jnp.float32,
        )
        for h in range(head_count)
    ])
    own_pairs = jnp.stack([
        lax.dot_general(
            queries[:, h * HD:(h + 1) * HD], grad_rows[:, h * HD:(h + 1) * HD],
            (((0,), (0,)), ((), ())), preferred_element_type=jnp.float32,
        )
        for h in range(head_count)
    ])
    position = lax.axis_index(SEQ)
    level_count = seq_count.bit_length() - 1
    inflow = jnp.zeros_like(own_state)
    outflow = jnp.zeros_like(own_state)
    totals = jnp.stack([own_state, own_pairs])
    level = 0
    while level < level_count:
        if seq_count == 64 and level == 2:
            group = position >> level & 3
            gathered = totals
            for shift in range(1, 4):
                route = []
                for i in range(seq_count):
                    mine = i >> level & 3
                    target = i - (mine << level) + ((mine + shift) % 4 << level)
                    route.append((i, target))
                other = lax.ppermute(totals.astype(jnp.bfloat16), SEQ, route).astype(jnp.float32)
                source = (group - shift) % 4
                inflow = inflow + jnp.where(source < group, other[0], 0.0)
                outflow = outflow + jnp.where(source > group, other[1], 0.0)
                gathered = gathered + other
            totals = gathered
            level += 2
            continue
        other = swapped(totals.astype(jnp.bfloat16), seq_count, level).astype(jnp.float32)
        upper_half = position >> level & 1 == 1
        inflow = inflow + jnp.where(upper_half, other[0], 0.0)
        outflow = outflow + jnp.where(upper_half, 0.0, other[1])
        totals = totals + other
        level += 1
    before = inflow[None] + jnp.cumsum(key_value, 0) - key_value
    later_state = outflow[None] + own_pairs[None] - jnp.cumsum(query_pairs, 0)
    before_parts = split_state(before)
    later_parts = split_state(later_state)
    scores = jnp.einsum(
        "cthd,cshd->chts", query_blocks, key_blocks, preferred_element_type=jnp.float32
    )
    weights = jnp.where(causal, factor * scores, 0.0).astype(jnp.bfloat16)
    within = jnp.einsum(
        "chts,cshe->cthe", weights, value_blocks, preferred_element_type=jnp.float32
    )
    carried = factor * state_product("cthd,chde->cthe", query_blocks, before_parts)
    attention = (within + carried).astype(jnp.bfloat16).reshape(flat_shape)
    partial_output = lax.dot_general(
        attention, out_weight, (((1,), (1,)), ((), ())), preferred_element_type=jnp.float32
    ).astype(jnp.bfloat16)
    partial_output, attention = lax.optimization_barrier((partial_output, attention))
    output = lax.psum_scatter(partial_output, "head", scatter_dimension=0, tiled=True)
    weight_partial = lax.dot_general(
        out_grad, attention, (((0,), (0,)), ((), ())), preferred_element_type=jnp.float32
    )
    if seq_count == 64:
        weight_grad, (before_parts, later_parts) = grid_scatter(
            weight_partial, 4, 8, (before_parts, later_parts)
        )
    else:
        weight_grad = halving_scatter(weight_partial, seq_count)
    grad_scores = jnp.einsum(
        "cthe,cshe->chts", grad_blocks, value_blocks, preferred_element_type=jnp.float32
    )
    grad_weights = jnp.where(causal, factor * grad_scores, 0.0).astype(jnp.bfloat16)
    query_grad = jnp.einsum(
        "chts,cshd->cthd", grad_weights, key_blocks, preferred_element_type=jnp.float32
    )
    query_grad = query_grad + factor * state_product("cthe,chde->cthd", grad_blocks, before_parts)
    key_grad = jnp.einsum(
        "chts,cthd->cshd", grad_weights, query_blocks, preferred_element_type=jnp.float32
    )
    key_grad = key_grad + factor * state_product("cshe,chde->cshd", value_blocks, later_parts)
    value_grad = jnp.einsum(
        "chts,cthe->cshe", weights, grad_blocks, preferred_element_type=jnp.float32
    )
    value_grad = value_grad + factor * state_product("cshd,chde->cshe", key_blocks, later_parts)
    weight_grad = weight_grad * total_rows ** (-0.5)
    return (
        output,
        query_grad.astype(jnp.bfloat16).reshape(flat_shape),
        key_grad.astype(jnp.bfloat16).reshape(flat_shape),
        value_grad.astype(jnp.bfloat16).reshape(flat_shape),
        weight_grad,
    )


def solution(mesh):
    seq_count, head_count_axis = mesh.devices.shape
    split_mesh = Mesh(
        mesh.devices.reshape(seq_count // 2, 2, head_count_axis), ("xy", "c", "head")
    )

    def body(queries, key_rows, value_rows, out_weight, out_grad):
        return local(queries, key_rows, value_rows, out_weight, out_grad, seq_count, head_count_axis)

    return jax.shard_map(
        body,
        mesh=split_mesh,
        in_specs=(
            P(SEQ, "head"),
            P(SEQ, "head"),
            P(SEQ, "head"),
            P(None, "head"),
            P(SEQ, None),
        ),
        out_specs=(
            P(SEQ + ("head",), None),
            P(SEQ, "head"),
            P(SEQ, "head"),
            P(SEQ, "head"),
            P(SEQ, "head"),
        ),
        check_vma=False,
    )
```

```python
import jax
import jax.numpy as jnp
from jax import lax
from jax.sharding import Mesh
from jax.sharding import PartitionSpec as P

HD = 128
CH = 64
SEQ = ("xy", "c")


def swapped(block, count, distance):
    route = []
    for low in range(count):
        high = low | 1 << distance
        if high != low and high < count:
            route += [(low, high), (high, low)]
    return lax.ppermute(block, SEQ, route)


def split_state(state):
    upper = state.astype(jnp.bfloat16)
    lower = (state - upper.astype(jnp.float32)).astype(jnp.bfloat16)
    return (upper, lower)


def state_product(form, operand, parts):
    first = jnp.einsum(form, operand, parts[0], preferred_element_type=jnp.float32)
    return first + jnp.einsum(form, operand, parts[1], preferred_element_type=jnp.float32)


def halving_order(bits):
    if bits != 6:
        return list(range(bits))
    return [0, 1, 4, 2, 5, 3]


def halving_scatter(partial, count):
    bits = count.bit_length() - 1
    position = lax.axis_index(SEQ)
    cols = partial.shape[1]
    acc = partial.reshape((2,) * bits + (partial.shape[0] // count, cols))
    held = list(range(bits - 1, -1, -1))
    for bit in halving_order(bits):
        axis = held.index(bit)
        mine = position >> bit & 1
        lower = lax.index_in_dim(acc, 0, axis, keepdims=False)
        upper = lax.index_in_dim(acc, 1, axis, keepdims=False)
        kept = jnp.where(mine == 1, upper, lower)
        sent = jnp.where(mine == 1, lower, upper)
        route = [(i, i ^ 1 << bit) for i in range(count)]
        acc = kept + lax.ppermute(sent, SEQ, route)
        held.pop(axis)
    return acc.reshape(-1, cols)


def wire(block, route):
    return lax.ppermute(block.astype(jnp.bfloat16), SEQ, route).astype(jnp.float32)


def grid_scatter(partial, x_count, y_count, ride):
    count = x_count * y_count * 2
    cols = partial.shape[1]
    position = lax.axis_index(SEQ)
    core = position % 2
    y = position // 2 % y_count
    x = position // (2 * y_count)
    index = lambda a, b, c: a * 2 * y_count + b % y_count * 2 + c
    acc = partial.reshape(x_count, y_count, 2, partial.shape[0] // count, cols)
    kept = lax.dynamic_index_in_dim(acc, core, 2, keepdims=False)
    sent = lax.dynamic_index_in_dim(acc, 1 - core, 2, keepdims=False)
    acc = kept + lax.ppermute(sent, SEQ, [(i, i ^ 1) for i in range(count)])
    acc, ride = lax.optimization_barrier((acc, ride))
    acc = jnp.where(core == 1, jnp.roll(acc, -1, axis=1), acc)
    acc = acc.reshape(x_count, y_count // 2, 2, acc.shape[2], cols)
    label = (y - core) % y_count
    odd = label % 2
    route = []
    for a in range(x_count):
        for b in range(y_count):
            for c in range(2):
                other = ((b - c) % y_count ^ 1) + c
                route.append((index(a, b, c), index(a, other, c)))
    kept = lax.dynamic_index_in_dim(acc, odd, 2, keepdims=False)
    sent = lax.dynamic_index_in_dim(acc, 1 - odd, 2, keepdims=False)
    acc = kept + wire(sent, route)
    total = lax.dynamic_index_in_dim(acc, x, 0, keepdims=False)
    for shift in range(1, x_count):
        piece = lax.dynamic_index_in_dim(acc, (x + shift) % x_count, 0, keepdims=False)
        route = [(index(a, b, c), index((a + shift) % x_count, b, c))
                 for a in range(x_count) for b in range(y_count) for c in range(2)]
        total = total + wire(piece, route)
    acc = total
    quarter = label // 2
    groups = y_count // 2
    total = lax.dynamic_index_in_dim(acc, quarter, 0, keepdims=False)
    for shift in range(1, groups):
        piece = lax.dynamic_index_in_dim(acc, (quarter + shift) % groups, 0, keepdims=False)
        route = [(index(a, b, c), index(a, b + 2 * shift, c))
                 for a in range(x_count) for b in range(y_count) for c in range(2)]
        total = total + wire(piece, route)
    return total, ride


def local(queries, key_rows, value_rows, out_weight, out_grad, seq_count, head_count_axis):
    local_rows = queries.shape[0]
    head_count = queries.shape[1] // HD
    blocks = local_rows // CH
    total_rows = local_rows * seq_count
    factor = (HD * total_rows) ** (-0.5)
    block_shape = (blocks, CH, head_count, HD)
    flat_shape = (local_rows, head_count * HD)
    query_blocks = queries.reshape(block_shape)
    key_blocks = key_rows.reshape(block_shape)
    value_blocks = value_rows.reshape(block_shape)
    causal = (jnp.arange(CH)[:, None] >= jnp.arange(CH)[None, :])[None, None]
    grad_rows = jnp.dot(out_grad, out_weight, preferred_element_type=jnp.float32).astype(
        jnp.bfloat16
    )
    grad_blocks = grad_rows.reshape(block_shape)
    key_value = jnp.einsum(
        "cshd,cshe->chde", key_blocks, value_blocks, preferred_element_type=jnp.float32
    )
    query_pairs = jnp.einsum(
        "cthd,cthe->chde", query_blocks, grad_blocks, preferred_element_type=jnp.float32
    )
    own_state = jnp.stack([
        lax.dot_general(
            key_rows[:, h * HD:(h + 1) * HD], value_rows[:, h * HD:(h + 1) * HD],
            (((0,), (0,)), ((), ())), preferred_element_type=jnp.float32,
        )
        for h in range(head_count)
    ])
    own_pairs = jnp.stack([
        lax.dot_general(
            queries[:, h * HD:(h + 1) * HD], grad_rows[:, h * HD:(h + 1) * HD],
            (((0,), (0,)), ((), ())), preferred_element_type=jnp.float32,
        )
        for h in range(head_count)
    ])
    position = lax.axis_index(SEQ)
    level_count = seq_count.bit_length() - 1
    inflow = jnp.zeros_like(own_state)
    outflow = jnp.zeros_like(own_state)
    totals = jnp.stack([own_state, own_pairs])
    level = 0
    while level < level_count:
        if seq_count == 64 and level == 2:
            group = position >> level & 3
            gathered = totals
            for shift in range(1, 4):
                route = []
                for i in range(seq_count):
                    mine = i >> level & 3
                    target = i - (mine << level) + ((mine + shift) % 4 << level)
                    route.append((i, target))
                other = lax.ppermute(totals.astype(jnp.bfloat16), SEQ, route).astype(jnp.float32)
                source = (group - shift) % 4
                inflow = inflow + jnp.where(source < group, other[0], 0.0)
                outflow = outflow + jnp.where(source > group, other[1], 0.0)
                gathered = gathered + other
            totals = gathered
            level += 2
            continue
        other = swapped(totals.astype(jnp.bfloat16), seq_count, level).astype(jnp.float32)
        upper_half = position >> level & 1 == 1
        inflow = inflow + jnp.where(upper_half, other[0], 0.0)
        outflow = outflow + jnp.where(upper_half, 0.0, other[1])
        totals = totals + other
        level += 1
    local_before = split_state(jnp.cumsum(key_value, 0) - key_value)
    local_later = split_state(own_pairs[None] - jnp.cumsum(query_pairs, 0))
    inflow_parts = split_state(inflow)
    outflow_parts = split_state(outflow)
    scores = jnp.einsum(
        "cthd,cshd->chts", query_blocks, key_blocks, preferred_element_type=jnp.float32
    )
    weights = jnp.where(causal, factor * scores, 0.0).astype(jnp.bfloat16)
    within = jnp.einsum(
        "chts,cshe->cthe", weights, value_blocks, preferred_element_type=jnp.float32
    )
    carried = factor * (
        state_product("cthd,chde->cthe", query_blocks, local_before)
        + state_product("cthd,hde->cthe", query_blocks, inflow_parts)
    )
    attention = (within + carried).astype(jnp.bfloat16).reshape(flat_shape)
    partial_output = lax.dot_general(
        attention, out_weight, (((1,), (1,)), ((), ())), preferred_element_type=jnp.float32
    ).astype(jnp.bfloat16)
    partial_output, attention = lax.optimization_barrier((partial_output, attention))
    output = lax.psum_scatter(partial_output, "head", scatter_dimension=0, tiled=True)
    weight_partial = lax.dot_general(
        out_grad, attention, (((0,), (0,)), ((), ())), preferred_element_type=jnp.float32
    )
    if seq_count == 64:
        weight_grad, (inflow_parts, outflow_parts) = grid_scatter(
            weight_partial, 4, 8, (inflow_parts, outflow_parts)
        )
    else:
        weight_grad = halving_scatter(weight_partial, seq_count)
    grad_scores = jnp.einsum(
        "cthe,cshe->chts", grad_blocks, value_blocks, preferred_element_type=jnp.float32
    )
    grad_weights = jnp.where(causal, factor * grad_scores, 0.0).astype(jnp.bfloat16)
    query_grad = jnp.einsum(
        "chts,cshd->cthd", grad_weights, key_blocks, preferred_element_type=jnp.float32
    )
    query_grad = query_grad + factor * (
        state_product("cthe,chde->cthd", grad_blocks, local_before)
        + state_product("cthe,hde->cthd", grad_blocks, inflow_parts)
    )
    key_grad = jnp.einsum(
        "chts,cthd->cshd", grad_weights, query_blocks, preferred_element_type=jnp.float32
    )
    key_grad = key_grad + factor * (
        state_product("cshe,chde->cshd", value_blocks, local_later)
        + state_product("cshe,hde->cshd", value_blocks, outflow_parts)
    )
    value_grad = jnp.einsum(
        "chts,cthe->cshe", weights, grad_blocks, preferred_element_type=jnp.float32
    )
    value_grad = value_grad + factor * (
        state_product("cshd,chde->cshe", key_blocks, local_later)
        + state_product("cshd,hde->cshe", key_blocks, outflow_parts)
    )
    weight_grad = weight_grad * total_rows ** (-0.5)
    return (
        output,
        query_grad.astype(jnp.bfloat16).reshape(flat_shape),
        key_grad.astype(jnp.bfloat16).reshape(flat_shape),
        value_grad.astype(jnp.bfloat16).reshape(flat_shape),
        weight_grad,
    )


def solution(mesh):
    seq_count, head_count_axis = mesh.devices.shape
    split_mesh = Mesh(
        mesh.devices.reshape(seq_count // 2, 2, head_count_axis), ("xy", "c", "head")
    )

    def body(queries, key_rows, value_rows, out_weight, out_grad):
        return local(queries, key_rows, value_rows, out_weight, out_grad, seq_count, head_count_axis)

    return jax.shard_map(
        body,
        mesh=split_mesh,
        in_specs=(
            P(SEQ, "head"),
            P(SEQ, "head"),
            P(SEQ, "head"),
            P(None, "head"),
            P(SEQ, None),
        ),
        out_specs=(
            P(SEQ + ("head",), None),
            P(SEQ, "head"),
            P(SEQ, "head"),
            P(SEQ, "head"),
            P(SEQ, "head"),
        ),
        check_vma=False,
    )
```

```python
import jax
import jax.numpy as jnp
from jax import lax
from jax.sharding import Mesh
from jax.sharding import PartitionSpec as P

HD = 128
CH = 64
SEQ = ("xy", "c")


def swapped(block, count, distance):
    route = []
    for low in range(count):
        high = low | 1 << distance
        if high != low and high < count:
            route += [(low, high), (high, low)]
    return lax.ppermute(block, SEQ, route)


def masked(keep, block):
    return jnp.where(keep, block, jnp.zeros_like(block)).astype(jnp.float32)


def split_state(state):
    upper = state.astype(jnp.bfloat16)
    lower = (state - upper.astype(jnp.float32)).astype(jnp.bfloat16)
    return (upper, lower)


def state_product(form, operand, parts):
    first = jnp.einsum(form, operand, parts[0], preferred_element_type=jnp.float32)
    return first + jnp.einsum(form, operand, parts[1], preferred_element_type=jnp.float32)


def halving_order(bits):
    if bits != 6:
        return list(range(bits))
    return [0, 1, 4, 2, 5, 3]


def halving_scatter(partial, count):
    bits = count.bit_length() - 1
    position = lax.axis_index(SEQ)
    cols = partial.shape[1]
    acc = partial.reshape((2,) * bits + (partial.shape[0] // count, cols))
    held = list(range(bits - 1, -1, -1))
    for bit in halving_order(bits):
        axis = held.index(bit)
        mine = position >> bit & 1
        lower = lax.index_in_dim(acc, 0, axis, keepdims=False)
        upper = lax.index_in_dim(acc, 1, axis, keepdims=False)
        kept = jnp.where(mine == 1, upper, lower)
        sent = jnp.where(mine == 1, lower, upper)
        route = [(i, i ^ 1 << bit) for i in range(count)]
        acc = kept + lax.ppermute(sent, SEQ, route)
        held.pop(axis)
    return acc.reshape(-1, cols)


def wire(block, route):
    return lax.ppermute(block.astype(jnp.bfloat16), SEQ, route).astype(jnp.float32)


def grid_scatter(partial, x_count, y_count, ride):
    count = x_count * y_count * 2
    cols = partial.shape[1]
    position = lax.axis_index(SEQ)
    core = position % 2
    y = position // 2 % y_count
    x = position // (2 * y_count)
    index = lambda a, b, c: a * 2 * y_count + b % y_count * 2 + c
    acc = partial.reshape(x_count, y_count, 2, partial.shape[0] // count, cols)
    kept = lax.dynamic_index_in_dim(acc, core, 2, keepdims=False)
    sent = lax.dynamic_index_in_dim(acc, 1 - core, 2, keepdims=False)
    acc = kept + lax.ppermute(sent, SEQ, [(i, i ^ 1) for i in range(count)])
    acc, ride = lax.optimization_barrier((acc, ride))
    acc = jnp.where(core == 1, jnp.roll(acc, -1, axis=1), acc)
    acc = acc.reshape(x_count, y_count // 2, 2, acc.shape[2], cols)
    label = (y - core) % y_count
    odd = label % 2
    route = []
    for a in range(x_count):
        for b in range(y_count):
            for c in range(2):
                other = ((b - c) % y_count ^ 1) + c
                route.append((index(a, b, c), index(a, other, c)))
    kept = lax.dynamic_index_in_dim(acc, odd, 2, keepdims=False)
    sent = lax.dynamic_index_in_dim(acc, 1 - odd, 2, keepdims=False)
    acc = kept + wire(sent, route)
    total = lax.dynamic_index_in_dim(acc, x, 0, keepdims=False)
    for shift in range(1, x_count):
        piece = lax.dynamic_index_in_dim(acc, (x + shift) % x_count, 0, keepdims=False)
        route = [(index(a, b, c), index((a + shift) % x_count, b, c))
                 for a in range(x_count) for b in range(y_count) for c in range(2)]
        total = total + wire(piece, route)
    acc = total
    quarter = label // 2
    groups = y_count // 2
    total = lax.dynamic_index_in_dim(acc, quarter, 0, keepdims=False)
    for shift in range(1, groups):
        piece = lax.dynamic_index_in_dim(acc, (quarter + shift) % groups, 0, keepdims=False)
        route = [(index(a, b, c), index(a, b + 2 * shift, c))
                 for a in range(x_count) for b in range(y_count) for c in range(2)]
        total = total + wire(piece, route)
    return total, ride


def local(queries, key_rows, value_rows, out_weight, out_grad, seq_count, head_count_axis):
    local_rows = queries.shape[0]
    head_count = queries.shape[1] // HD
    blocks = local_rows // CH
    total_rows = local_rows * seq_count
    factor = (HD * total_rows) ** (-0.5)
    block_shape = (blocks, CH, head_count, HD)
    flat_shape = (local_rows, head_count * HD)
    query_blocks = queries.reshape(block_shape)
    key_blocks = key_rows.reshape(block_shape)
    value_blocks = value_rows.reshape(block_shape)
    causal = (jnp.arange(CH)[:, None] >= jnp.arange(CH)[None, :])[None, None]
    grad_rows = jnp.dot(out_grad, out_weight, preferred_element_type=jnp.float32).astype(
        jnp.bfloat16
    )
    grad_blocks = grad_rows.reshape(block_shape)
    key_value = jnp.einsum(
        "cshd,cshe->chde", key_blocks, value_blocks, preferred_element_type=jnp.float32
    )
    query_pairs = jnp.einsum(
        "cthd,cthe->chde", query_blocks, grad_blocks, preferred_element_type=jnp.float32
    )
    own_state = jnp.stack([
        lax.dot_general(
            key_rows[:, h * HD:(h + 1) * HD], value_rows[:, h * HD:(h + 1) * HD],
            (((0,), (0,)), ((), ())), preferred_element_type=jnp.float32,
        )
        for h in range(head_count)
    ])
    own_pairs = jnp.stack([
        lax.dot_general(
            queries[:, h * HD:(h + 1) * HD], grad_rows[:, h * HD:(h + 1) * HD],
            (((0,), (0,)), ((), ())), preferred_element_type=jnp.float32,
        )
        for h in range(head_count)
    ])
    position = lax.axis_index(SEQ)
    level_count = seq_count.bit_length() - 1
    inflow = jnp.zeros_like(own_state)
    outflow = jnp.zeros_like(own_state)
    totals = jnp.stack([own_state, own_pairs])
    level = 0
    while level < level_count:
        if seq_count == 64 and level == 2:
            group = position >> level & 3
            gathered = totals
            for shift in range(1, 4):
                route = []
                for i in range(seq_count):
                    mine = i >> level & 3
                    target = i - (mine << level) + ((mine + shift) % 4 << level)
                    route.append((i, target))
                other = lax.ppermute(totals.astype(jnp.bfloat16), SEQ, route)
                source = (group - shift) % 4
                inflow = inflow + masked(source < group, other[0])
                outflow = outflow + masked(source > group, other[1])
                gathered = gathered + other.astype(jnp.float32)
            totals = gathered
            level += 2
            continue
        other = swapped(totals.astype(jnp.bfloat16), seq_count, level)
        upper_half = position >> level & 1 == 1
        inflow = inflow + masked(upper_half, other[0])
        outflow = outflow + masked(~upper_half, other[1])
        totals = totals + other.astype(jnp.float32)
        level += 1
    before = inflow[None] + jnp.cumsum(key_value, 0) - key_value
    later_state = outflow[None] + own_pairs[None] - jnp.cumsum(query_pairs, 0)
    before_parts = split_state(before)
    later_parts = split_state(later_state)
    scores = jnp.einsum(
        "cthd,cshd->chts", query_blocks, key_blocks, preferred_element_type=jnp.float32
    )
    weights = jnp.where(causal, factor * scores, 0.0).astype(jnp.bfloat16)
    within = jnp.einsum(
        "chts,cshe->cthe", weights, value_blocks, preferred_element_type=jnp.float32
    )
    carried = factor * state_product("cthd,chde->cthe", query_blocks, before_parts)
    attention = (within + carried).astype(jnp.bfloat16).reshape(flat_shape)
    partial_output = lax.dot_general(
        attention, out_weight, (((1,), (1,)), ((), ())), preferred_element_type=jnp.float32
    ).astype(jnp.bfloat16)
    partial_output, attention = lax.optimization_barrier((partial_output, attention))
    output = lax.psum_scatter(partial_output, "head", scatter_dimension=0, tiled=True)
    weight_partial = lax.dot_general(
        out_grad, attention, (((0,), (0,)), ((), ())), preferred_element_type=jnp.float32
    )
    if seq_count == 64:
        weight_grad, (before_parts, later_parts) = grid_scatter(
            weight_partial, 4, 8, (before_parts, later_parts)
        )
    else:
        weight_grad = halving_scatter(weight_partial, seq_count)
    grad_scores = jnp.einsum(
        "cthe,cshe->chts", grad_blocks, value_blocks, preferred_element_type=jnp.float32
    )
    grad_weights = jnp.where(causal, factor * grad_scores, 0.0).astype(jnp.bfloat16)
    query_grad = jnp.einsum(
        "chts,cshd->cthd", grad_weights, key_blocks, preferred_element_type=jnp.float32
    )
    query_grad = query_grad + factor * state_product("cthe,chde->cthd", grad_blocks, before_parts)
    key_grad = jnp.einsum(
        "chts,cthd->cshd", grad_weights, query_blocks, preferred_element_type=jnp.float32
    )
    key_grad = key_grad + factor * state_product("cshe,chde->cshd", value_blocks, later_parts)
    value_grad = jnp.einsum(
        "chts,cthe->cshe", weights, grad_blocks, preferred_element_type=jnp.float32
    )
    value_grad = value_grad + factor * state_product("cshd,chde->cshe", key_blocks, later_parts)
    weight_grad = weight_grad * total_rows ** (-0.5)
    return (
        output,
        query_grad.astype(jnp.bfloat16).reshape(flat_shape),
        key_grad.astype(jnp.bfloat16).reshape(flat_shape),
        value_grad.astype(jnp.bfloat16).reshape(flat_shape),
        weight_grad,
    )


def solution(mesh):
    seq_count, head_count_axis = mesh.devices.shape
    split_mesh = Mesh(
        mesh.devices.reshape(seq_count // 2, 2, head_count_axis), ("xy", "c", "head")
    )

    def body(queries, key_rows, value_rows, out_weight, out_grad):
        return local(queries, key_rows, value_rows, out_weight, out_grad, seq_count, head_count_axis)

    return jax.shard_map(
        body,
        mesh=split_mesh,
        in_specs=(
            P(SEQ, "head"),
            P(SEQ, "head"),
            P(SEQ, "head"),
            P(None, "head"),
            P(SEQ, None),
        ),
        out_specs=(
            P(SEQ + ("head",), None),
            P(SEQ, "head"),
            P(SEQ, "head"),
            P(SEQ, "head"),
            P(SEQ, "head"),
        ),
        check_vma=False,
    )
```

```python
import jax
import jax.numpy as jnp
from jax import lax
from jax.sharding import Mesh
from jax.sharding import PartitionSpec as P

HD = 128
CH = 64
SEQ = ("xy", "c")


def swapped(block, count, distance):
    route = []
    for low in range(count):
        high = low | 1 << distance
        if high != low and high < count:
            route += [(low, high), (high, low)]
    return lax.ppermute(block, SEQ, route)


def masked(keep, block):
    return jnp.where(keep, block, jnp.zeros_like(block)).astype(jnp.float32)


def split_state(state):
    upper = state.astype(jnp.bfloat16)
    lower = (state - upper.astype(jnp.float32)).astype(jnp.bfloat16)
    return (upper, lower)


def state_product(form, operand, parts):
    first = jnp.einsum(form, operand, parts[0], preferred_element_type=jnp.float32)
    return first + jnp.einsum(form, operand, parts[1], preferred_element_type=jnp.float32)


def halving_order(bits):
    if bits != 6:
        return list(range(bits))
    return [0, 1, 4, 2, 5, 3]


def halving_scatter(partial, count):
    bits = count.bit_length() - 1
    position = lax.axis_index(SEQ)
    cols = partial.shape[1]
    acc = partial.reshape((2,) * bits + (partial.shape[0] // count, cols))
    held = list(range(bits - 1, -1, -1))
    for bit in halving_order(bits):
        axis = held.index(bit)
        mine = position >> bit & 1
        lower = lax.index_in_dim(acc, 0, axis, keepdims=False)
        upper = lax.index_in_dim(acc, 1, axis, keepdims=False)
        kept = jnp.where(mine == 1, upper, lower)
        sent = jnp.where(mine == 1, lower, upper)
        route = [(i, i ^ 1 << bit) for i in range(count)]
        acc = kept + lax.ppermute(sent, SEQ, route)
        held.pop(axis)
    return acc.reshape(-1, cols)


def wire(block, route):
    return lax.ppermute(block.astype(jnp.bfloat16), SEQ, route).astype(jnp.float32)


def grid_scatter(partial, x_count, y_count, ride):
    count = x_count * y_count * 2
    position = lax.axis_index(SEQ)
    core = position % 2
    y = position // 2 % y_count
    x = position // (2 * y_count)
    index = lambda a, b, c: a * 2 * y_count + b % y_count * 2 + c
    cols = partial.shape[0]
    half = partial.shape[1] // 2
    kept = lax.dynamic_slice_in_dim(partial, core * half, half, 1)
    sent = lax.dynamic_slice_in_dim(partial, (1 - core) * half, half, 1)
    acc = kept + lax.ppermute(sent, SEQ, [(i, i ^ 1) for i in range(count)])
    acc = acc.reshape(cols, x_count, y_count, half // (x_count * y_count)).transpose(1, 2, 3, 0)
    acc, ride = lax.optimization_barrier((acc, ride))
    acc = jnp.where(core == 1, jnp.roll(acc, -1, axis=1), acc)
    acc = acc.reshape(x_count, y_count // 2, 2, acc.shape[2], cols)
    label = (y - core) % y_count
    odd = label % 2
    route = []
    for a in range(x_count):
        for b in range(y_count):
            for c in range(2):
                other = ((b - c) % y_count ^ 1) + c
                route.append((index(a, b, c), index(a, other, c)))
    kept = lax.dynamic_index_in_dim(acc, odd, 2, keepdims=False)
    sent = lax.dynamic_index_in_dim(acc, 1 - odd, 2, keepdims=False)
    acc = kept + wire(sent, route)
    total = lax.dynamic_index_in_dim(acc, x, 0, keepdims=False)
    for shift in range(1, x_count):
        piece = lax.dynamic_index_in_dim(acc, (x + shift) % x_count, 0, keepdims=False)
        route = [(index(a, b, c), index((a + shift) % x_count, b, c))
                 for a in range(x_count) for b in range(y_count) for c in range(2)]
        total = total + wire(piece, route)
    acc = total
    quarter = label // 2
    groups = y_count // 2
    total = lax.dynamic_index_in_dim(acc, quarter, 0, keepdims=False)
    for shift in range(1, groups):
        piece = lax.dynamic_index_in_dim(acc, (quarter + shift) % groups, 0, keepdims=False)
        route = [(index(a, b, c), index(a, b + 2 * shift, c))
                 for a in range(x_count) for b in range(y_count) for c in range(2)]
        total = total + wire(piece, route)
    return total, ride


def local(queries, key_rows, value_rows, out_weight, out_grad, seq_count, head_count_axis):
    local_rows = queries.shape[0]
    head_count = queries.shape[1] // HD
    blocks = local_rows // CH
    total_rows = local_rows * seq_count
    factor = (HD * total_rows) ** (-0.5)
    block_shape = (blocks, CH, head_count, HD)
    flat_shape = (local_rows, head_count * HD)
    query_blocks = queries.reshape(block_shape)
    key_blocks = key_rows.reshape(block_shape)
    value_blocks = value_rows.reshape(block_shape)
    causal = (jnp.arange(CH)[:, None] >= jnp.arange(CH)[None, :])[None, None]
    grad_rows = jnp.dot(out_grad, out_weight, preferred_element_type=jnp.float32).astype(
        jnp.bfloat16
    )
    grad_blocks = grad_rows.reshape(block_shape)
    key_value = jnp.einsum(
        "cshd,cshe->chde", key_blocks, value_blocks, preferred_element_type=jnp.float32
    )
    query_pairs = jnp.einsum(
        "cthd,cthe->chde", query_blocks, grad_blocks, preferred_element_type=jnp.float32
    )
    own_state = jnp.stack([
        lax.dot_general(
            key_rows[:, h * HD:(h + 1) * HD], value_rows[:, h * HD:(h + 1) * HD],
            (((0,), (0,)), ((), ())), preferred_element_type=jnp.float32,
        )
        for h in range(head_count)
    ])
    own_pairs = jnp.stack([
        lax.dot_general(
            queries[:, h * HD:(h + 1) * HD], grad_rows[:, h * HD:(h + 1) * HD],
            (((0,), (0,)), ((), ())), preferred_element_type=jnp.float32,
        )
        for h in range(head_count)
    ])
    position = lax.axis_index(SEQ)
    level_count = seq_count.bit_length() - 1
    inflow = jnp.zeros_like(own_state)
    outflow = jnp.zeros_like(own_state)
    totals = jnp.stack([own_state, own_pairs])
    level = 0
    while level < level_count:
        if seq_count == 64 and level == 2:
            group = position >> level & 3
            gathered = totals
            for shift in range(1, 4):
                route = []
                for i in range(seq_count):
                    mine = i >> level & 3
                    target = i - (mine << level) + ((mine + shift) % 4 << level)
                    route.append((i, target))
                other = lax.ppermute(totals.astype(jnp.bfloat16), SEQ, route)
                source = (group - shift) % 4
                inflow = inflow + masked(source < group, other[0])
                outflow = outflow + masked(source > group, other[1])
                gathered = gathered + other.astype(jnp.float32)
            totals = gathered
            level += 2
            continue
        other = swapped(totals.astype(jnp.bfloat16), seq_count, level)
        upper_half = position >> level & 1 == 1
        inflow = inflow + masked(upper_half, other[0])
        outflow = outflow + masked(~upper_half, other[1])
        totals = totals + other.astype(jnp.float32)
        level += 1
    before = inflow[None] + jnp.cumsum(key_value, 0) - key_value
    later_state = outflow[None] + own_pairs[None] - jnp.cumsum(query_pairs, 0)
    before_parts = split_state(before)
    later_parts = split_state(later_state)
    scores = jnp.einsum(
        "cthd,cshd->chts", query_blocks, key_blocks, preferred_element_type=jnp.float32
    )
    weights = jnp.where(causal, factor * scores, 0.0).astype(jnp.bfloat16)
    within = jnp.einsum(
        "chts,cshe->cthe", weights, value_blocks, preferred_element_type=jnp.float32
    )
    carried = factor * state_product("cthd,chde->cthe", query_blocks, before_parts)
    attention = (within + carried).astype(jnp.bfloat16).reshape(flat_shape)
    partial_output = lax.dot_general(
        attention, out_weight, (((1,), (1,)), ((), ())), preferred_element_type=jnp.float32
    ).astype(jnp.bfloat16)
    partial_output, attention = lax.optimization_barrier((partial_output, attention))
    output = lax.psum_scatter(partial_output, "head", scatter_dimension=0, tiled=True)
    if seq_count == 64:
        block = out_grad.shape[1] // seq_count
        reordered = out_grad.reshape(local_rows, seq_count // 2, 2, block)
        reordered = reordered.transpose(0, 2, 1, 3).reshape(local_rows, -1)
        flipped = lax.dot_general(
            attention, reordered, (((0,), (0,)), ((), ())), preferred_element_type=jnp.float32
        )
        weight_grad, (before_parts, later_parts) = grid_scatter(
            flipped, 4, 8, (before_parts, later_parts)
        )
    else:
        weight_partial = lax.dot_general(
            out_grad, attention, (((0,), (0,)), ((), ())), preferred_element_type=jnp.float32
        )
        weight_grad = halving_scatter(weight_partial, seq_count)
    grad_scores = jnp.einsum(
        "cthe,cshe->chts", grad_blocks, value_blocks, preferred_element_type=jnp.float32
    )
    grad_weights = jnp.where(causal, factor * grad_scores, 0.0).astype(jnp.bfloat16)
    query_grad = jnp.einsum(
        "chts,cshd->cthd", grad_weights, key_blocks, preferred_element_type=jnp.float32
    )
    query_grad = query_grad + factor * state_product("cthe,chde->cthd", grad_blocks, before_parts)
    key_grad = jnp.einsum(
        "chts,cthd->cshd", grad_weights, query_blocks, preferred_element_type=jnp.float32
    )
    key_grad = key_grad + factor * state_product("cshe,chde->cshd", value_blocks, later_parts)
    value_grad = jnp.einsum(
        "chts,cthe->cshe", weights, grad_blocks, preferred_element_type=jnp.float32
    )
    value_grad = value_grad + factor * state_product("cshd,chde->cshe", key_blocks, later_parts)
    weight_grad = weight_grad * total_rows ** (-0.5)
    return (
        output,
        query_grad.astype(jnp.bfloat16).reshape(flat_shape),
        key_grad.astype(jnp.bfloat16).reshape(flat_shape),
        value_grad.astype(jnp.bfloat16).reshape(flat_shape),
        weight_grad,
    )


def solution(mesh):
    seq_count, head_count_axis = mesh.devices.shape
    split_mesh = Mesh(
        mesh.devices.reshape(seq_count // 2, 2, head_count_axis), ("xy", "c", "head")
    )

    def body(queries, key_rows, value_rows, out_weight, out_grad):
        return local(queries, key_rows, value_rows, out_weight, out_grad, seq_count, head_count_axis)

    return jax.shard_map(
        body,
        mesh=split_mesh,
        in_specs=(
            P(SEQ, "head"),
            P(SEQ, "head"),
            P(SEQ, "head"),
            P(None, "head"),
            P(SEQ, None),
        ),
        out_specs=(
            P(SEQ + ("head",), None),
            P(SEQ, "head"),
            P(SEQ, "head"),
            P(SEQ, "head"),
            P(SEQ, "head"),
        ),
        check_vma=False,
    )
```

```python
import jax
import jax.numpy as jnp
from jax import lax
from jax.sharding import Mesh
from jax.sharding import PartitionSpec as P

HD = 128
CH = 64
SEQ = ("xy", "c")


def swapped(block, count, distance):
    route = []
    for low in range(count):
        high = low | 1 << distance
        if high != low and high < count:
            route += [(low, high), (high, low)]
    return lax.ppermute(block, SEQ, route)


def split_state(state):
    upper = state.astype(jnp.bfloat16)
    lower = (state - upper.astype(jnp.float32)).astype(jnp.bfloat16)
    return (upper, lower)


def state_product(form, operand, parts):
    first = jnp.einsum(form, operand, parts[0], preferred_element_type=jnp.float32)
    return first + jnp.einsum(form, operand, parts[1], preferred_element_type=jnp.float32)


def halving_order(bits):
    if bits != 6:
        return list(range(bits))
    return [0, 1, 4, 2, 5, 3]


def halving_scatter(partial, count):
    bits = count.bit_length() - 1
    position = lax.axis_index(SEQ)
    cols = partial.shape[1]
    acc = partial.reshape((2,) * bits + (partial.shape[0] // count, cols))
    held = list(range(bits - 1, -1, -1))
    for bit in halving_order(bits):
        axis = held.index(bit)
        mine = position >> bit & 1
        lower = lax.index_in_dim(acc, 0, axis, keepdims=False)
        upper = lax.index_in_dim(acc, 1, axis, keepdims=False)
        kept = jnp.where(mine == 1, upper, lower)
        sent = jnp.where(mine == 1, lower, upper)
        route = [(i, i ^ 1 << bit) for i in range(count)]
        acc = kept + lax.ppermute(sent, SEQ, route)
        held.pop(axis)
    return acc.reshape(-1, cols)


def wire(block, route):
    return lax.ppermute(block.astype(jnp.bfloat16), SEQ, route).astype(jnp.float32)


def grid_scatter(partial, x_count, y_count, ride):
    count = x_count * y_count * 2
    cols = partial.shape[1]
    position = lax.axis_index(SEQ)
    core = position % 2
    y = position // 2 % y_count
    x = position // (2 * y_count)
    index = lambda a, b, c: a * 2 * y_count + b % y_count * 2 + c
    acc = partial.reshape(x_count, y_count, 2, partial.shape[0] // count, cols)
    kept = lax.dynamic_index_in_dim(acc, core, 2, keepdims=False)
    sent = lax.dynamic_index_in_dim(acc, 1 - core, 2, keepdims=False)
    acc = kept + lax.ppermute(sent, SEQ, [(i, i ^ 1) for i in range(count)])
    acc, ride = lax.optimization_barrier((acc, ride))
    acc = jnp.where(core == 1, jnp.roll(acc, -1, axis=1), acc)
    acc = acc.reshape(x_count, y_count // 2, 2, acc.shape[2], cols)
    label = (y - core) % y_count
    odd = label % 2
    route = []
    for a in range(x_count):
        for b in range(y_count):
            for c in range(2):
                other = ((b - c) % y_count ^ 1) + c
                route.append((index(a, b, c), index(a, other, c)))
    kept = lax.dynamic_index_in_dim(acc, odd, 2, keepdims=False)
    sent = lax.dynamic_index_in_dim(acc, 1 - odd, 2, keepdims=False)
    acc = kept + wire(sent, route)
    total = lax.dynamic_index_in_dim(acc, x, 0, keepdims=False)
    for shift in range(1, x_count):
        piece = lax.dynamic_index_in_dim(acc, (x + shift) % x_count, 0, keepdims=False)
        route = [(index(a, b, c), index((a + shift) % x_count, b, c))
                 for a in range(x_count) for b in range(y_count) for c in range(2)]
        total = total + wire(piece, route)
    acc = total
    quarter = label // 2
    groups = y_count // 2
    total = lax.dynamic_index_in_dim(acc, quarter, 0, keepdims=False)
    for shift in range(1, groups):
        piece = lax.dynamic_index_in_dim(acc, (quarter + shift) % groups, 0, keepdims=False)
        route = [(index(a, b, c), index(a, b + 2 * shift, c))
                 for a in range(x_count) for b in range(y_count) for c in range(2)]
        total = total + wire(piece, route)
    return total, ride


def local(queries, key_rows, value_rows, out_weight, out_grad, seq_count, head_count_axis):
    local_rows = queries.shape[0]
    head_count = queries.shape[1] // HD
    blocks = local_rows // CH
    total_rows = local_rows * seq_count
    factor = (HD * total_rows) ** (-0.5)
    block_shape = (blocks, CH, head_count, HD)
    flat_shape = (local_rows, head_count * HD)
    query_blocks = queries.reshape(block_shape)
    key_blocks = key_rows.reshape(block_shape)
    value_blocks = value_rows.reshape(block_shape)
    causal = (jnp.arange(CH)[:, None] >= jnp.arange(CH)[None, :])[None, None]
    grad_rows = jnp.dot(out_grad, out_weight, preferred_element_type=jnp.float32).astype(
        jnp.bfloat16
    )
    grad_blocks = grad_rows.reshape(block_shape)
    key_value = jnp.einsum(
        "cshd,cshe->chde", key_blocks, value_blocks, preferred_element_type=jnp.float32
    )
    query_pairs = jnp.einsum(
        "cthd,cthe->chde", query_blocks, grad_blocks, preferred_element_type=jnp.float32
    )
    own_state = jnp.stack([
        lax.dot_general(
            key_rows[:, h * HD:(h + 1) * HD], value_rows[:, h * HD:(h + 1) * HD],
            (((0,), (0,)), ((), ())), preferred_element_type=jnp.float32,
        )
        for h in range(head_count)
    ])
    own_pairs = jnp.stack([
        lax.dot_general(
            queries[:, h * HD:(h + 1) * HD], grad_rows[:, h * HD:(h + 1) * HD],
            (((0,), (0,)), ((), ())), preferred_element_type=jnp.float32,
        )
        for h in range(head_count)
    ])
    position = lax.axis_index(SEQ)
    level_count = seq_count.bit_length() - 1
    inflow = jnp.zeros_like(own_state)
    outflow = jnp.zeros_like(own_state)
    totals = jnp.stack([own_state, own_pairs])
    for level in range(level_count):
        other = swapped(totals.astype(jnp.bfloat16), seq_count, level).astype(jnp.float32)
        upper_half = position >> level & 1 == 1
        inflow = inflow + jnp.where(upper_half, other[0], 0.0)
        outflow = outflow + jnp.where(upper_half, 0.0, other[1])
        totals = totals + other
    before = inflow[None] + jnp.cumsum(key_value, 0) - key_value
    later_state = outflow[None] + own_pairs[None] - jnp.cumsum(query_pairs, 0)
    before_parts = split_state(before)
    later_parts = split_state(later_state)
    scores = jnp.einsum(
        "cthd,cshd->chts", query_blocks, key_blocks, preferred_element_type=jnp.float32
    )
    weights = jnp.where(causal, factor * scores, 0.0).astype(jnp.bfloat16)
    within = jnp.einsum(
        "chts,cshe->cthe", weights, value_blocks, preferred_element_type=jnp.float32
    )
    carried = factor * state_product("cthd,chde->cthe", query_blocks, before_parts)
    attention = (within + carried).astype(jnp.bfloat16).reshape(flat_shape)
    partial_output = lax.dot_general(
        attention, out_weight, (((1,), (1,)), ((), ())), preferred_element_type=jnp.float32
    ).astype(jnp.bfloat16)
    partial_output, attention = lax.optimization_barrier((partial_output, attention))
    output = lax.psum_scatter(partial_output, "head", scatter_dimension=0, tiled=True)
    weight_partial = lax.dot_general(
        out_grad, attention, (((0,), (0,)), ((), ())), preferred_element_type=jnp.float32
    )
    if seq_count == 64:
        weight_grad, (inflow, outflow) = grid_scatter(weight_partial, 4, 8, (inflow, outflow))
        before_parts = split_state(inflow[None] + jnp.cumsum(key_value, 0) - key_value)
        later_parts = split_state(outflow[None] + own_pairs[None] - jnp.cumsum(query_pairs, 0))
    else:
        weight_grad = halving_scatter(weight_partial, seq_count)
    grad_scores = jnp.einsum(
        "cthe,cshe->chts", grad_blocks, value_blocks, preferred_element_type=jnp.float32
    )
    grad_weights = jnp.where(causal, factor * grad_scores, 0.0).astype(jnp.bfloat16)
    query_grad = jnp.einsum(
        "chts,cshd->cthd", grad_weights, key_blocks, preferred_element_type=jnp.float32
    )
    query_grad = query_grad + factor * state_product("cthe,chde->cthd", grad_blocks, before_parts)
    key_grad = jnp.einsum(
        "chts,cthd->cshd", grad_weights, query_blocks, preferred_element_type=jnp.float32
    )
    key_grad = key_grad + factor * state_product("cshe,chde->cshd", value_blocks, later_parts)
    value_grad = jnp.einsum(
        "chts,cthe->cshe", weights, grad_blocks, preferred_element_type=jnp.float32
    )
    value_grad = value_grad + factor * state_product("cshd,chde->cshe", key_blocks, later_parts)
    weight_grad = weight_grad * total_rows ** (-0.5)
    return (
        output,
        query_grad.astype(jnp.bfloat16).reshape(flat_shape),
        key_grad.astype(jnp.bfloat16).reshape(flat_shape),
        value_grad.astype(jnp.bfloat16).reshape(flat_shape),
        weight_grad,
    )


def solution(mesh):
    seq_count, head_count_axis = mesh.devices.shape
    split_mesh = Mesh(
        mesh.devices.reshape(seq_count // 2, 2, head_count_axis), ("xy", "c", "head")
    )

    def body(queries, key_rows, value_rows, out_weight, out_grad):
        return local(queries, key_rows, value_rows, out_weight, out_grad, seq_count, head_count_axis)

    return jax.shard_map(
        body,
        mesh=split_mesh,
        in_specs=(
            P(SEQ, "head"),
            P(SEQ, "head"),
            P(SEQ, "head"),
            P(None, "head"),
            P(SEQ, None),
        ),
        out_specs=(
            P(SEQ + ("head",), None),
            P(SEQ, "head"),
            P(SEQ, "head"),
            P(SEQ, "head"),
            P(SEQ, "head"),
        ),
        check_vma=False,
    )
```

```python
import jax
import jax.numpy as jnp
from jax import lax
from jax.sharding import Mesh
from jax.sharding import PartitionSpec as P

HD = 128
CH = 64
SEQ = ("xy", "c")


def swapped(block, count, distance):
    route = []
    for low in range(count):
        high = low | 1 << distance
        if high != low and high < count:
            route += [(low, high), (high, low)]
    return lax.ppermute(block, SEQ, route)


def split_state(state):
    upper = state.astype(jnp.bfloat16)
    lower = (state - upper.astype(jnp.float32)).astype(jnp.bfloat16)
    return (upper, lower)


def state_product(form, operand, parts):
    first = jnp.einsum(form, operand, parts[0], preferred_element_type=jnp.float32)
    return first + jnp.einsum(form, operand, parts[1], preferred_element_type=jnp.float32)


def halving_order(bits):
    if bits != 6:
        return list(range(bits))
    return [0, 1, 4, 2, 5, 3]


def halving_scatter(partial, count):
    bits = count.bit_length() - 1
    position = lax.axis_index(SEQ)
    cols = partial.shape[1]
    acc = partial.reshape((2,) * bits + (partial.shape[0] // count, cols))
    held = list(range(bits - 1, -1, -1))
    for bit in halving_order(bits):
        axis = held.index(bit)
        mine = position >> bit & 1
        lower = lax.index_in_dim(acc, 0, axis, keepdims=False)
        upper = lax.index_in_dim(acc, 1, axis, keepdims=False)
        kept = jnp.where(mine == 1, upper, lower)
        sent = jnp.where(mine == 1, lower, upper)
        route = [(i, i ^ 1 << bit) for i in range(count)]
        acc = kept + lax.ppermute(sent, SEQ, route)
        held.pop(axis)
    return acc.reshape(-1, cols)


def wire(block, route):
    return lax.ppermute(block.astype(jnp.bfloat16), SEQ, route).astype(jnp.float32)


def grid_scatter(partial, x_count, y_count, ride):
    count = x_count * y_count * 2
    cols = partial.shape[1]
    position = lax.axis_index(SEQ)
    core = position % 2
    y = position // 2 % y_count
    x = position // (2 * y_count)
    index = lambda a, b, c: a * 2 * y_count + b % y_count * 2 + c
    acc = partial.reshape(x_count, y_count, 2, partial.shape[0] // count, cols)
    kept = jnp.roll(lax.dynamic_index_in_dim(acc, core, 2, keepdims=False), -core, axis=1)
    sent = jnp.roll(lax.dynamic_index_in_dim(acc, 1 - core, 2, keepdims=False), core - 1, axis=1)
    acc = kept + lax.ppermute(sent, SEQ, [(i, i ^ 1) for i in range(count)])
    acc, ride = lax.optimization_barrier((acc, ride))
    acc = acc.reshape(x_count, y_count // 2, 2, acc.shape[2], cols)
    label = (y - core) % y_count
    odd = label % 2
    route = []
    for a in range(x_count):
        for b in range(y_count):
            for c in range(2):
                other = ((b - c) % y_count ^ 1) + c
                route.append((index(a, b, c), index(a, other, c)))
    kept = lax.dynamic_index_in_dim(acc, odd, 2, keepdims=False)
    sent = lax.dynamic_index_in_dim(acc, 1 - odd, 2, keepdims=False)
    acc = kept + wire(sent, route)
    total = lax.dynamic_index_in_dim(acc, x, 0, keepdims=False)
    for shift in range(1, x_count):
        piece = lax.dynamic_index_in_dim(acc, (x + shift) % x_count, 0, keepdims=False)
        route = [(index(a, b, c), index((a + shift) % x_count, b, c))
                 for a in range(x_count) for b in range(y_count) for c in range(2)]
        total = total + wire(piece, route)
    acc = total
    quarter = label // 2
    groups = y_count // 2
    total = lax.dynamic_index_in_dim(acc, quarter, 0, keepdims=False)
    for shift in range(1, groups):
        piece = lax.dynamic_index_in_dim(acc, (quarter + shift) % groups, 0, keepdims=False)
        route = [(index(a, b, c), index(a, b + 2 * shift, c))
                 for a in range(x_count) for b in range(y_count) for c in range(2)]
        total = total + wire(piece, route)
    return total, ride


def local(queries, key_rows, value_rows, out_weight, out_grad, seq_count, head_count_axis):
    local_rows = queries.shape[0]
    head_count = queries.shape[1] // HD
    blocks = local_rows // CH
    total_rows = local_rows * seq_count
    factor = (HD * total_rows) ** (-0.5)
    block_shape = (blocks, CH, head_count, HD)
    flat_shape = (local_rows, head_count * HD)
    query_blocks = queries.reshape(block_shape)
    key_blocks = key_rows.reshape(block_shape)
    value_blocks = value_rows.reshape(block_shape)
    causal = (jnp.arange(CH)[:, None] >= jnp.arange(CH)[None, :])[None, None]
    grad_rows = jnp.dot(out_grad, out_weight, preferred_element_type=jnp.float32).astype(
        jnp.bfloat16
    )
    grad_blocks = grad_rows.reshape(block_shape)
    key_value = jnp.einsum(
        "cshd,cshe->chde", key_blocks, value_blocks, preferred_element_type=jnp.float32
    )
    query_pairs = jnp.einsum(
        "cthd,cthe->chde", query_blocks, grad_blocks, preferred_element_type=jnp.float32
    )
    own_state = jnp.stack([
        lax.dot_general(
            key_rows[:, h * HD:(h + 1) * HD], value_rows[:, h * HD:(h + 1) * HD],
            (((0,), (0,)), ((), ())), preferred_element_type=jnp.float32,
        )
        for h in range(head_count)
    ])
    own_pairs = jnp.stack([
        lax.dot_general(
            queries[:, h * HD:(h + 1) * HD], grad_rows[:, h * HD:(h + 1) * HD],
            (((0,), (0,)), ((), ())), preferred_element_type=jnp.float32,
        )
        for h in range(head_count)
    ])
    position = lax.axis_index(SEQ)
    level_count = seq_count.bit_length() - 1
    inflow = jnp.zeros_like(own_state)
    outflow = jnp.zeros_like(own_state)
    totals = jnp.stack([own_state, own_pairs])
    for level in range(level_count):
        other = swapped(totals.astype(jnp.bfloat16), seq_count, level).astype(jnp.float32)
        upper_half = position >> level & 1 == 1
        inflow = inflow + jnp.where(upper_half, other[0], 0.0)
        outflow = outflow + jnp.where(upper_half, 0.0, other[1])
        totals = totals + other
    before = inflow[None] + jnp.cumsum(key_value, 0) - key_value
    later_state = outflow[None] + own_pairs[None] - jnp.cumsum(query_pairs, 0)
    before_parts = split_state(before)
    later_parts = split_state(later_state)
    scores = jnp.einsum(
        "cthd,cshd->chts", query_blocks, key_blocks, preferred_element_type=jnp.float32
    )
    weights = jnp.where(causal, factor * scores, 0.0).astype(jnp.bfloat16)
    within = jnp.einsum(
        "chts,cshe->cthe", weights, value_blocks, preferred_element_type=jnp.float32
    )
    carried = factor * state_product("cthd,chde->cthe", query_blocks, before_parts)
    attention = (within + carried).astype(jnp.bfloat16).reshape(flat_shape)
    partial_output = lax.dot_general(
        attention, out_weight, (((1,), (1,)), ((), ())), preferred_element_type=jnp.float32
    ).astype(jnp.bfloat16)
    partial_output, attention = lax.optimization_barrier((partial_output, attention))
    output = lax.psum_scatter(partial_output, "head", scatter_dimension=0, tiled=True)
    weight_partial = lax.dot_general(
        out_grad, attention, (((0,), (0,)), ((), ())), preferred_element_type=jnp.float32
    )
    if seq_count == 64:
        weight_grad, (before_parts, later_parts) = grid_scatter(
            weight_partial, 4, 8, (before_parts, later_parts)
        )
    else:
        weight_grad = halving_scatter(weight_partial, seq_count)
    grad_scores = jnp.einsum(
        "cthe,cshe->chts", grad_blocks, value_blocks, preferred_element_type=jnp.float32
    )
    grad_weights = jnp.where(causal, factor * grad_scores, 0.0).astype(jnp.bfloat16)
    query_grad = jnp.einsum(
        "chts,cshd->cthd", grad_weights, key_blocks, preferred_element_type=jnp.float32
    )
    query_grad = query_grad + factor * state_product("cthe,chde->cthd", grad_blocks, before_parts)
    key_grad = jnp.einsum(
        "chts,cthd->cshd", grad_weights, query_blocks, preferred_element_type=jnp.float32
    )
    key_grad = key_grad + factor * state_product("cshe,chde->cshd", value_blocks, later_parts)
    value_grad = jnp.einsum(
        "chts,cthe->cshe", weights, grad_blocks, preferred_element_type=jnp.float32
    )
    value_grad = value_grad + factor * state_product("cshd,chde->cshe", key_blocks, later_parts)
    weight_grad = weight_grad * total_rows ** (-0.5)
    return (
        output,
        query_grad.astype(jnp.bfloat16).reshape(flat_shape),
        key_grad.astype(jnp.bfloat16).reshape(flat_shape),
        value_grad.astype(jnp.bfloat16).reshape(flat_shape),
        weight_grad,
    )


def solution(mesh):
    seq_count, head_count_axis = mesh.devices.shape
    split_mesh = Mesh(
        mesh.devices.reshape(seq_count // 2, 2, head_count_axis), ("xy", "c", "head")
    )

    def body(queries, key_rows, value_rows, out_weight, out_grad):
        return local(queries, key_rows, value_rows, out_weight, out_grad, seq_count, head_count_axis)

    return jax.shard_map(
        body,
        mesh=split_mesh,
        in_specs=(
            P(SEQ, "head"),
            P(SEQ, "head"),
            P(SEQ, "head"),
            P(None, "head"),
            P(SEQ, None),
        ),
        out_specs=(
            P(SEQ + ("head",), None),
            P(SEQ, "head"),
            P(SEQ, "head"),
            P(SEQ, "head"),
            P(SEQ, "head"),
        ),
        check_vma=False,
    )
```

```python
import jax
import jax.numpy as jnp
from jax import lax
from jax.sharding import Mesh
from jax.sharding import PartitionSpec as P

HD = 128
CH = 64
SEQ = ("xy", "c")


def swapped(block, count, distance):
    route = []
    for low in range(count):
        high = low | 1 << distance
        if high != low and high < count:
            route += [(low, high), (high, low)]
    return lax.ppermute(block, SEQ, route)


def split_state(state):
    upper = state.astype(jnp.bfloat16)
    lower = (state - upper.astype(jnp.float32)).astype(jnp.bfloat16)
    return (upper, lower)


def state_product(form, operand, parts):
    first = jnp.einsum(form, operand, parts[0], preferred_element_type=jnp.float32)
    return first + jnp.einsum(form, operand, parts[1], preferred_element_type=jnp.float32)


def halving_order(bits):
    if bits != 6:
        return list(range(bits))
    return [0, 1, 4, 2, 5, 3]


def halving_scatter(partial, count):
    bits = count.bit_length() - 1
    position = lax.axis_index(SEQ)
    cols = partial.shape[1]
    acc = partial.reshape((2,) * bits + (partial.shape[0] // count, cols))
    held = list(range(bits - 1, -1, -1))
    for bit in halving_order(bits):
        axis = held.index(bit)
        mine = position >> bit & 1
        lower = lax.index_in_dim(acc, 0, axis, keepdims=False)
        upper = lax.index_in_dim(acc, 1, axis, keepdims=False)
        kept = jnp.where(mine == 1, upper, lower)
        sent = jnp.where(mine == 1, lower, upper)
        route = [(i, i ^ 1 << bit) for i in range(count)]
        acc = kept + lax.ppermute(sent, SEQ, route)
        held.pop(axis)
    return acc.reshape(-1, cols)


def wire(block, route):
    return lax.ppermute(block.astype(jnp.bfloat16), SEQ, route).astype(jnp.float32)


def grid_scatter(partial, x_count, y_count, ride):
    count = x_count * y_count * 2
    cols = partial.shape[1]
    position = lax.axis_index(SEQ)
    core = position % 2
    y = position // 2 % y_count
    x = position // (2 * y_count)
    index = lambda a, b, c: a * 2 * y_count + b % y_count * 2 + c
    acc = partial.reshape(x_count, y_count, 2, partial.shape[0] // count, cols)
    sent = lax.dynamic_index_in_dim(acc, 1 - core, 2, keepdims=False)
    kept = lax.dynamic_index_in_dim(lax.optimization_barrier(acc), core, 2, keepdims=False)
    acc = kept + lax.ppermute(sent, SEQ, [(i, i ^ 1) for i in range(count)])
    acc, ride = lax.optimization_barrier((acc, ride))
    acc = jnp.where(core == 1, jnp.roll(acc, -1, axis=1), acc)
    acc = acc.reshape(x_count, y_count // 2, 2, acc.shape[2], cols)
    label = (y - core) % y_count
    odd = label % 2
    route = []
    for a in range(x_count):
        for b in range(y_count):
            for c in range(2):
                other = ((b - c) % y_count ^ 1) + c
                route.append((index(a, b, c), index(a, other, c)))
    kept = lax.dynamic_index_in_dim(acc, odd, 2, keepdims=False)
    sent = lax.dynamic_index_in_dim(acc, 1 - odd, 2, keepdims=False)
    acc = kept + wire(sent, route)
    total = lax.dynamic_index_in_dim(acc, x, 0, keepdims=False)
    for shift in range(1, x_count):
        piece = lax.dynamic_index_in_dim(acc, (x + shift) % x_count, 0, keepdims=False)
        route = [(index(a, b, c), index((a + shift) % x_count, b, c))
                 for a in range(x_count) for b in range(y_count) for c in range(2)]
        total = total + wire(piece, route)
    acc = total
    quarter = label // 2
    groups = y_count // 2
    total = lax.dynamic_index_in_dim(acc, quarter, 0, keepdims=False)
    for shift in range(1, groups):
        piece = lax.dynamic_index_in_dim(acc, (quarter + shift) % groups, 0, keepdims=False)
        route = [(index(a, b, c), index(a, b + 2 * shift, c))
                 for a in range(x_count) for b in range(y_count) for c in range(2)]
        total = total + wire(piece, route)
    return total, ride


def local(queries, key_rows, value_rows, out_weight, out_grad, seq_count, head_count_axis):
    local_rows = queries.shape[0]
    head_count = queries.shape[1] // HD
    blocks = local_rows // CH
    total_rows = local_rows * seq_count
    factor = (HD * total_rows) ** (-0.5)
    block_shape = (blocks, CH, head_count, HD)
    flat_shape = (local_rows, head_count * HD)
    query_blocks = queries.reshape(block_shape)
    key_blocks = key_rows.reshape(block_shape)
    value_blocks = value_rows.reshape(block_shape)
    causal = (jnp.arange(CH)[:, None] >= jnp.arange(CH)[None, :])[None, None]
    grad_rows = jnp.dot(out_grad, out_weight, preferred_element_type=jnp.float32).astype(
        jnp.bfloat16
    )
    grad_blocks = grad_rows.reshape(block_shape)
    key_value = jnp.einsum(
        "cshd,cshe->chde", key_blocks, value_blocks, preferred_element_type=jnp.float32
    )
    query_pairs = jnp.einsum(
        "cthd,cthe->chde", query_blocks, grad_blocks, preferred_element_type=jnp.float32
    )
    own_state = jnp.stack([
        lax.dot_general(
            key_rows[:, h * HD:(h + 1) * HD], value_rows[:, h * HD:(h + 1) * HD],
            (((0,), (0,)), ((), ())), preferred_element_type=jnp.float32,
        )
        for h in range(head_count)
    ])
    own_pairs = jnp.stack([
        lax.dot_general(
            queries[:, h * HD:(h + 1) * HD], grad_rows[:, h * HD:(h + 1) * HD],
            (((0,), (0,)), ((), ())), preferred_element_type=jnp.float32,
        )
        for h in range(head_count)
    ])
    position = lax.axis_index(SEQ)
    level_count = seq_count.bit_length() - 1
    inflow = jnp.zeros_like(own_state)
    outflow = jnp.zeros_like(own_state)
    totals = jnp.stack([own_state, own_pairs])
    for level in range(level_count):
        other = swapped(totals.astype(jnp.bfloat16), seq_count, level).astype(jnp.float32)
        upper_half = position >> level & 1 == 1
        inflow = inflow + jnp.where(upper_half, other[0], 0.0)
        outflow = outflow + jnp.where(upper_half, 0.0, other[1])
        totals = totals + other
    before = inflow[None] + jnp.cumsum(key_value, 0) - key_value
    later_state = outflow[None] + own_pairs[None] - jnp.cumsum(query_pairs, 0)
    before_parts = split_state(before)
    later_parts = split_state(later_state)
    scores = jnp.einsum(
        "cthd,cshd->chts", query_blocks, key_blocks, preferred_element_type=jnp.float32
    )
    weights = jnp.where(causal, factor * scores, 0.0).astype(jnp.bfloat16)
    within = jnp.einsum(
        "chts,cshe->cthe", weights, value_blocks, preferred_element_type=jnp.float32
    )
    carried = factor * state_product("cthd,chde->cthe", query_blocks, before_parts)
    attention = (within + carried).astype(jnp.bfloat16).reshape(flat_shape)
    partial_output = lax.dot_general(
        attention, out_weight, (((1,), (1,)), ((), ())), preferred_element_type=jnp.float32
    ).astype(jnp.bfloat16)
    partial_output, attention = lax.optimization_barrier((partial_output, attention))
    output = lax.psum_scatter(partial_output, "head", scatter_dimension=0, tiled=True)
    weight_partial = lax.dot_general(
        out_grad, attention, (((0,), (0,)), ((), ())), preferred_element_type=jnp.float32
    )
    if seq_count == 64:
        weight_grad, (before_parts, later_parts) = grid_scatter(
            weight_partial, 4, 8, (before_parts, later_parts)
        )
    else:
        weight_grad = halving_scatter(weight_partial, seq_count)
    grad_scores = jnp.einsum(
        "cthe,cshe->chts", grad_blocks, value_blocks, preferred_element_type=jnp.float32
    )
    grad_weights = jnp.where(causal, factor * grad_scores, 0.0).astype(jnp.bfloat16)
    query_grad = jnp.einsum(
        "chts,cshd->cthd", grad_weights, key_blocks, preferred_element_type=jnp.float32
    )
    query_grad = query_grad + factor * state_product("cthe,chde->cthd", grad_blocks, before_parts)
    key_grad = jnp.einsum(
        "chts,cthd->cshd", grad_weights, query_blocks, preferred_element_type=jnp.float32
    )
    key_grad = key_grad + factor * state_product("cshe,chde->cshd", value_blocks, later_parts)
    value_grad = jnp.einsum(
        "chts,cthe->cshe", weights, grad_blocks, preferred_element_type=jnp.float32
    )
    value_grad = value_grad + factor * state_product("cshd,chde->cshe", key_blocks, later_parts)
    weight_grad = weight_grad * total_rows ** (-0.5)
    return (
        output,
        query_grad.astype(jnp.bfloat16).reshape(flat_shape),
        key_grad.astype(jnp.bfloat16).reshape(flat_shape),
        value_grad.astype(jnp.bfloat16).reshape(flat_shape),
        weight_grad,
    )


def solution(mesh):
    seq_count, head_count_axis = mesh.devices.shape
    split_mesh = Mesh(
        mesh.devices.reshape(seq_count // 2, 2, head_count_axis), ("xy", "c", "head")
    )

    def body(queries, key_rows, value_rows, out_weight, out_grad):
        return local(queries, key_rows, value_rows, out_weight, out_grad, seq_count, head_count_axis)

    return jax.shard_map(
        body,
        mesh=split_mesh,
        in_specs=(
            P(SEQ, "head"),
            P(SEQ, "head"),
            P(SEQ, "head"),
            P(None, "head"),
            P(SEQ, None),
        ),
        out_specs=(
            P(SEQ + ("head",), None),
            P(SEQ, "head"),
            P(SEQ, "head"),
            P(SEQ, "head"),
            P(SEQ, "head"),
        ),
        check_vma=False,
    )
```
